32 devices in a mesh: crop: 8 (over z, y), head: 4 (over x, core).
Axes of the slice: x: 2, y: 2, z: 4, core: 2. Of those that a mesh axis runs over, the one named last changes fastest.
Arguments:
- global_rows: bfloat16 [4096, 4096], P('crop', 'head'), may hold values from -6 to 6
- crop_tokens: bfloat16 [8192, 4096], P('crop', 'head'), may hold values from -6 to 6
- query_weight: bfloat16 [4096, 4096], P('crop', 'head'), may hold values from -0.125 to 0.125
- key_weight: bfloat16 [4096, 4096], P('crop', 'head'), may hold values from -0.125 to 0.125
- value_weight: bfloat16 [4096, 4096], P('crop', 'head'), may hold values from -0.09375 to 0.09375
- fetch_slots: int32 [8, 8, 2], P('crop'), may hold values from 0 to 63
- region_slots: int32 [128, 8], P('crop'), may hold values from 0 to 15, as said below
- region_len: int32 [128], P('crop'), may hold values from 4 to 8
Outputs:
- attended: bfloat16 [4096, 4096], P('crop', 'head')
The draws below stay inside these ranges and needn't reach their ends.
Inputs may be any that keep to these rules, and one draw needn't show every extreme that they name: `fetch_slots`: entry [s, o, c] numbers one of the 64 crop blocks of index s of crop. `region_slots`: the blocks listed for one page-row are distinct; the lists of the 16 page-rows of one index of crop together name all 16 delivered blocks. page-row r uses its first region_len[r] listed blocks.
All inputs are finite; a program needn't handle non-finite values.
Results may differ from the reference program's by a relative error of at most 0.008.
Values may be sent and summed in bfloat16 or wider, within the bound.
No kernel may reach another device: no remote copies, remote signals or barrier semaphores. Data moves between devices by JAX's collectives and lax.ppermute only.
A program may use at most 128 MiB of HBM per device.

```python
import jax
import jax.numpy as jnp
from jax import lax

D = 4096
HEADS = 32
HD = 128
CT = 16
BLK_DEV = 64
CAP = 2
NB = 8
ROWS_DEV = 16
GR = 32
CROPS = 512
PAGEROWS = 128
SLOTS = 16
N_CROP = 8


def draw_region_slots(key, part):
    owners = PAGEROWS // ROWS_DEV
    keys = jax.random.split(jax.random.fold_in(key, 17), owners)
    perms = jax.vmap(lambda k: jax.random.permutation(k, SLOTS))(keys)
    position = (jnp.arange(ROWS_DEV)[:, None] * NB + jnp.arange(NB)[None, :]) % SLOTS
    chosen = perms[:, position]
    return chosen.reshape(owners * ROWS_DEV, NB).astype(jnp.int32)


def drawn_rows(key, count, salt):
    return jax.random.truncated_normal(jax.random.fold_in(key, salt + 1), -6.0, 6.0, (count, D), jnp.float32)


def draw_global_rows(key, part):
    return drawn_rows(key, PAGEROWS * GR, 11).astype(jnp.bfloat16)


def draw_crop_tokens(key, part):
    return drawn_rows(key, CROPS * CT, 21).astype(jnp.bfloat16)


def weight_draw(key, salt):
    return jax.random.truncated_normal(jax.random.fold_in(key, salt), -6.0, 6.0, (D, D), jnp.float32) * D ** (-0.5)


def draw_query_weight(key, part):
    return weight_draw(key, 31).astype(jnp.bfloat16)


def draw_key_weight(key, part):
    return weight_draw(key, 32).astype(jnp.bfloat16)


def plant(entries, key, smallest, high):
    longest = entries.shape.index(max(entries.shape))
    spots = []
    for shift in (0, 1):
        where = [jax.random.randint(jax.random.fold_in(key, axis), (), 0, length) for axis, length in enumerate(entries.shape)]
        where[longest] = (where[longest] + shift) % entries.shape[longest]
        spots.append(tuple(where))
    return entries.at[spots[0]].set(smallest).at[spots[1]].set(high)


def steps_of(stream_key, shape, shards, low, largest):
    level, own = 1.0, jax.random.fold_in(stream_key, 6)
    for dim, blocks in shards:
        steps = jnp.exp(jax.random.uniform(jax.random.fold_in(own, dim), (blocks,), jnp.float32, low / len(shards), largest / len(shards)))
        level = level * jnp.repeat(steps, shape[dim] // blocks).reshape([-1 if axis == dim else 1 for axis in range(len(shape))])
    return level


def bell_draw(own_key, extent, spread, reach, cuts=(), kind=jnp.bfloat16):
    values = jax.random.normal(own_key, extent, jnp.float32) * spread
    if len(cuts) > 0:
        values = steps_of(own_key, extent, cuts, -0.22, 0.18) * values
    return jnp.clip(values, min=-reach, max=reach).astype(kind)


def setup_inputs(seed: int = 0) -> dict:
    key_of = jax.random.split(jax.random.key(seed), 9)
    global_rows = draw_global_rows(jax.random.fold_in(key_of[8], 71), 0)
    crop_tokens = draw_crop_tokens(jax.random.fold_in(key_of[8], 71), 0)
    query_weight = draw_query_weight(jax.random.fold_in(key_of[8], 71), 0)
    key_weight = draw_key_weight(jax.random.fold_in(key_of[8], 71), 0)
    value_weight = bell_draw(key_of[4], (D, D), D ** -0.5, 0.09375, ((0, 8), (1, 4)))
    fetch_slots = plant(jax.random.randint(key_of[5], (N_CROP, N_CROP, CAP), 0, BLK_DEV), jax.random.fold_in(key_of[5], 1), 0, BLK_DEV - 1).astype(jnp.int32)
    region_slots = draw_region_slots(jax.random.fold_in(key_of[8], 71), 0)
    region_len = plant(jax.random.randint(key_of[7], (PAGEROWS,), NB // 2, NB + 1), jax.random.fold_in(key_of[7], 1), NB // 2, NB).astype(jnp.int32)
    return {"global_rows": global_rows, "crop_tokens": crop_tokens, "query_weight": query_weight, "key_weight": key_weight, "value_weight": value_weight, "fetch_slots": fetch_slots, "region_slots": region_slots, "region_len": region_len}


def reference(global_rows, crop_tokens, query_weight, key_weight, value_weight, fetch_slots, region_slots, region_len):
    query = jnp.dot(global_rows, query_weight, preferred_element_type=jnp.float32).astype(jnp.bfloat16)
    keys = jnp.dot(crop_tokens, key_weight, preferred_element_type=jnp.float32).astype(jnp.bfloat16)
    values = jnp.dot(crop_tokens, value_weight, preferred_element_type=jnp.float32).astype(jnp.bfloat16)
    keys_blk = keys.reshape(CROPS, CT, D)
    vals_blk = values.reshape(CROPS, CT, D)
    owners = PAGEROWS // ROWS_DEV
    scale = 1.0 / (HD ** 0.5)

    def per_owner(owner):
        sources = jnp.arange(owners, dtype=jnp.int32)
        local = jnp.take(fetch_slots, owner, axis=1)
        crop_ids = (sources[:, None] * BLK_DEV + local).reshape(-1)
        slots = lax.dynamic_slice_in_dim(region_slots, (owner * ROWS_DEV).astype(jnp.int32), ROWS_DEV, 0)
        lens = lax.dynamic_slice_in_dim(region_len, (owner * ROWS_DEV).astype(jnp.int32), ROWS_DEV, 0)
        ids = crop_ids[slots]
        kk = keys_blk[ids].reshape(ROWS_DEV, NB * CT, HEADS, HD).astype(jnp.float32)
        vv = vals_blk[ids].reshape(ROWS_DEV, NB * CT, HEADS, HD).astype(jnp.float32)
        qq = lax.dynamic_slice_in_dim(query, (owner * ROWS_DEV * GR).astype(jnp.int32), ROWS_DEV * GR, 0)
        qq = qq.reshape(ROWS_DEV, GR, HEADS, HD).astype(jnp.float32)
        scores = jnp.einsum("rghe,rkhe->rhgk", qq, kk) * scale
        used = (jnp.arange(NB * CT, dtype=jnp.int32) // CT)[None, :] < lens[:, None]
        scores = jnp.where(used[:, None, None, :], scores, jnp.float32(-1e30))
        top = jnp.max(scores, axis=-1, keepdims=True)
        expo = jnp.exp(scores - top)
        weights = (expo / jnp.sum(expo, axis=-1, keepdims=True)).astype(jnp.bfloat16)
        result = jnp.einsum("rhgk,rkhe->rghe", weights.astype(jnp.float32), vv)
        return result.astype(jnp.bfloat16).reshape(ROWS_DEV * GR, D)

    stacked = lax.map(per_owner, jnp.arange(owners, dtype=jnp.int32))
    return stacked.reshape(PAGEROWS * GR, D)
```

```python
import jax
import jax.numpy as jnp
from jax import lax
from jax.sharding import PartitionSpec as P

HD = 128
CT = 16
CAP = 2
NB = 8
GR = 32


def ring_order(n):
    half = n // 2
    return [2 * i for i in range(half)] + [2 * i + 1 for i in reversed(range(half))]


def body(
    global_rows,
    crop_tokens,
    query_weight,
    key_weight,
    value_weight,
    fetch_slots,
    region_slots,
    region_len,
):
    width = key_weight.shape[1]
    wrows = key_weight.shape[0]
    heads_here = width // HD
    ncrop = lax.axis_size("crop")
    rows_here = region_slots.shape[0]

    ring = ring_order(ncrop)
    pos_of = [0] * ncrop
    for i, c in enumerate(ring):
        pos_of[c] = i
    me = lax.axis_index("crop")
    pos = jnp.array(pos_of, jnp.int32)[me]
    ring_arr = jnp.array(ring, jnp.int32)
    fwd_perm = [(ring[i], ring[(i + 1) % ncrop]) for i in range(ncrop)]
    bwd_perm = [(ring[i], ring[(i - 1) % ncrop]) for i in range(ncrop)]

    queries_in = lax.all_gather(global_rows, "head", axis=1, tiled=True)
    picks = fetch_slots[0]
    blocks = crop_tokens.reshape(-1, CT, crop_tokens.shape[1])
    chosen = blocks[picks].reshape(-1, crop_tokens.shape[1])
    tokens_in = lax.all_gather(chosen, "head", axis=1, tiled=True)

    stacked = jnp.concatenate([query_weight, key_weight, value_weight], axis=1)

    acc_q = jnp.zeros((queries_in.shape[0], width), jnp.float32)
    acc_kv = jnp.zeros((tokens_in.shape[0], 2 * width), jnp.float32)

    def contrib(acc_q, acc_kv, piece, src, lo, n):
        start = src * wrows + lo
        fq = lax.dynamic_slice_in_dim(queries_in, start, n, 1)
        ft = lax.dynamic_slice_in_dim(tokens_in, start, n, 1)
        acc_q = acc_q + jnp.dot(fq, piece[:, :width], preferred_element_type=jnp.float32)
        acc_kv = acc_kv + jnp.dot(ft, piece[:, width:], preferred_element_type=jnp.float32)
        return acc_q, acc_kv

    acc_q, acc_kv = contrib(acc_q, acc_kv, stacked, me, 0, wrows)
    steps_fwd = ncrop // 2
    steps_bwd = (ncrop - 1) // 2
    split = wrows // 2

    def ring_step(k, carry):
        fwd, bwd, acc_q, acc_kv = carry
        fwd = lax.ppermute(fwd, "crop", fwd_perm)
        bwd = lax.ppermute(bwd, "crop", bwd_perm)
        acc_q, acc_kv = contrib(acc_q, acc_kv, fwd, ring_arr[(pos - k) % ncrop], 0, wrows)
        acc_q, acc_kv = contrib(acc_q, acc_kv, bwd, ring_arr[(pos + k) % ncrop], 0, wrows)
        return fwd, bwd, acc_q, acc_kv

    fwd, bwd, acc_q, acc_kv = lax.fori_loop(
        1, steps_bwd + 1, ring_step, (stacked, stacked, acc_q, acc_kv)
    )
    if steps_fwd > steps_bwd:
        src = ring_arr[(pos - steps_fwd) % ncrop]
        fwd_piece = lax.ppermute(fwd[:split], "crop", fwd_perm)
        bwd_piece = lax.ppermute(bwd[split:], "crop", bwd_perm)
        acc_q, acc_kv = contrib(acc_q, acc_kv, fwd_piece, src, 0, split)
        acc_q, acc_kv = contrib(acc_q, acc_kv, bwd_piece, src, split, wrows - split)

    query = acc_q.astype(jnp.bfloat16)
    kv = acc_kv.astype(jnp.bfloat16)
    packed = kv.reshape(ncrop, CAP, CT, 2 * width)
    incoming = lax.all_to_all(packed, "crop", split_axis=0, concat_axis=0, tiled=True)
    slotted = incoming.reshape(ncrop * CAP, CT, 2 * width)
    listed = slotted[region_slots].reshape(rows_here, NB * CT, 2 * width)
    keys_row = listed[:, :, :width].reshape(rows_here, NB * CT, heads_here, HD)
    vals_row = listed[:, :, width:].reshape(rows_here, NB * CT, heads_here, HD)
    query_row = query.reshape(rows_here, GR, heads_here, HD)
    scale = 1.0 / HD**0.5
    scores = (
        jnp.einsum("rghe,rkhe->rhgk", query_row, keys_row, preferred_element_type=jnp.float32)
        * scale
    )
    used = (jnp.arange(NB * CT, dtype=jnp.int32) // CT)[None, :] < region_len[:, None]
    scores = jnp.where(used[:, None, None, :], scores, jnp.float32(-1e30))
    top = jnp.max(scores, axis=-1, keepdims=True)
    expo = jnp.exp(scores - top)
    weights = (expo / jnp.sum(expo, axis=-1, keepdims=True)).astype(jnp.bfloat16)
    result = jnp.einsum("rhgk,rkhe->rghe", weights, vals_row, preferred_element_type=jnp.float32)
    return result.astype(jnp.bfloat16).reshape(rows_here * GR, width)


def solution(mesh):
    placed = (
        P("crop", "head"),
        P("crop", "head"),
        P("crop", "head"),
        P("crop", "head"),
        P("crop", "head"),
        P("crop", None, None),
        P("crop", None),
        P("crop"),
    )
    return jax.shard_map(
        body, mesh=mesh, in_specs=placed, out_specs=P("crop", "head"), check_vma=False
    )
```

```python
import jax
import jax.numpy as jnp
from jax import lax
from jax.sharding import PartitionSpec as P

HD = 128
CT = 16
CAP = 2
NB = 8
GR = 32


def ring_order(n):
    half = n // 2
    return [2 * i for i in range(half)] + [2 * i + 1 for i in reversed(range(half))]


def body(
    global_rows,
    crop_tokens,
    query_weight,
    key_weight,
    value_weight,
    fetch_slots,
    region_slots,
    region_len,
):
    width = key_weight.shape[1]
    wrows = key_weight.shape[0]
    heads_here = width // HD
    ncrop = lax.axis_size("crop")
    rows_here = region_slots.shape[0]

    ring = ring_order(ncrop)
    pos_of = [0] * ncrop
    for i, c in enumerate(ring):
        pos_of[c] = i
    me = lax.axis_index("crop")
    pos = jnp.array(pos_of, jnp.int32)[me]
    ring_arr = jnp.array(ring, jnp.int32)
    fwd_perm = [(ring[i], ring[(i + 1) % ncrop]) for i in range(ncrop)]
    bwd_perm = [(ring[i], ring[(i - 1) % ncrop]) for i in range(ncrop)]

    queries_in = lax.all_gather(global_rows, "head", axis=1, tiled=True)
    picks = fetch_slots[0]
    blocks = crop_tokens.reshape(-1, CT, crop_tokens.shape[1])
    chosen = blocks[picks].reshape(-1, crop_tokens.shape[1])
    tokens_in = lax.all_gather(chosen, "head", axis=1, tiled=True)

    steps_fwd = ncrop // 2
    steps_bwd = (ncrop - 1) // 2
    split = wrows // 2

    def ring_gather(piece):
        buf = jnp.zeros((ncrop,) + piece.shape, piece.dtype)
        buf = lax.dynamic_update_slice(buf, piece[None], (me, 0, 0))

        def ring_step(k, carry):
            fwd, bwd, buf = carry
            fwd = lax.ppermute(fwd, "crop", fwd_perm)
            bwd = lax.ppermute(bwd, "crop", bwd_perm)
            buf = lax.dynamic_update_slice(buf, fwd[None], (ring_arr[(pos - k) % ncrop], 0, 0))
            buf = lax.dynamic_update_slice(buf, bwd[None], (ring_arr[(pos + k) % ncrop], 0, 0))
            return fwd, bwd, buf

        fwd, bwd, buf = lax.fori_loop(1, steps_bwd + 1, ring_step, (piece, piece, buf))
        if steps_fwd > steps_bwd:
            src = ring_arr[(pos - steps_fwd) % ncrop]
            top = lax.ppermute(fwd[:split], "crop", fwd_perm)
            bottom = lax.ppermute(bwd[split:], "crop", bwd_perm)
            buf = lax.dynamic_update_slice(buf, top[None], (src, 0, 0))
            buf = lax.dynamic_update_slice(buf, bottom[None], (src, split, 0))
        return buf.reshape(ncrop * wrows, piece.shape[1])

    kv_weight = ring_gather(jnp.concatenate([key_weight, value_weight], axis=1))
    kv = jnp.dot(tokens_in, kv_weight, preferred_element_type=jnp.float32).astype(jnp.bfloat16)
    packed = kv.reshape(ncrop, CAP, CT, 2 * width)
    incoming = lax.all_to_all(packed, "crop", split_axis=0, concat_axis=0, tiled=True)
    q_weight = ring_gather(query_weight)
    query = jnp.dot(queries_in, q_weight, preferred_element_type=jnp.float32).astype(jnp.bfloat16)
    slotted = incoming.reshape(ncrop * CAP, CT, 2 * width)
    listed = slotted[region_slots].reshape(rows_here, NB * CT, 2 * width)
    keys_row = listed[:, :, :width].reshape(rows_here, NB * CT, heads_here, HD)
    vals_row = listed[:, :, width:].reshape(rows_here, NB * CT, heads_here, HD)
    query_row = query.reshape(rows_here, GR, heads_here, HD)
    scale = 1.0 / HD**0.5
    scores = (
        jnp.einsum("rghe,rkhe->rhgk", query_row, keys_row, preferred_element_type=jnp.float32)
        * scale
    )
    used = (jnp.arange(NB * CT, dtype=jnp.int32) // CT)[None, :] < region_len[:, None]
    scores = jnp.where(used[:, None, None, :], scores, jnp.float32(-1e30))
    top = jnp.max(scores, axis=-1, keepdims=True)
    expo = jnp.exp(scores - top)
    weights = (expo / jnp.sum(expo, axis=-1, keepdims=True)).astype(jnp.bfloat16)
    result = jnp.einsum("rhgk,rkhe->rghe", weights, vals_row, preferred_element_type=jnp.float32)
    return result.astype(jnp.bfloat16).reshape(rows_here * GR, width)


def solution(mesh):
    placed = (
        P("crop", "head"),
        P("crop", "head"),
        P("crop", "head"),
        P("crop", "head"),
        P("crop", "head"),
        P("crop", None, None),
        P("crop", None),
        P("crop"),
    )
    return jax.shard_map(
        body, mesh=mesh, in_specs=placed, out_specs=P("crop", "head"), check_vma=False
    )
```

```python
import jax
import jax.numpy as jnp
from jax import lax
from jax.sharding import PartitionSpec as P

HD = 128
CT = 16
CAP = 2
NB = 8
GR = 32


def ring_order(n):
    half = n // 2
    return [2 * i for i in range(half)] + [2 * i + 1 for i in reversed(range(half))]


def body(
    global_rows,
    crop_tokens,
    query_weight,
    key_weight,
    value_weight,
    fetch_slots,
    region_slots,
    region_len,
):
    width = key_weight.shape[1]
    wrows = key_weight.shape[0]
    heads_here = width // HD
    ncrop = lax.axis_size("crop")
    rows_here = region_slots.shape[0]

    ring = ring_order(ncrop)
    pos_of = [0] * ncrop
    for i, c in enumerate(ring):
        pos_of[c] = i
    me = lax.axis_index("crop")
    pos = jnp.array(pos_of, jnp.int32)[me]
    ring_arr = jnp.array(ring, jnp.int32)
    fwd_perm = [(ring[i], ring[(i + 1) % ncrop]) for i in range(ncrop)]
    bwd_perm = [(ring[i], ring[(i - 1) % ncrop]) for i in range(ncrop)]

    queries_in = lax.all_gather(global_rows, "head", axis=1, tiled=True)
    picks = fetch_slots[0]
    blocks = crop_tokens.reshape(-1, CT, crop_tokens.shape[1])
    chosen = blocks[picks].reshape(-1, crop_tokens.shape[1])
    tokens_in = lax.all_gather(chosen, "head", axis=1, tiled=True)

    steps_fwd = ncrop // 2
    steps_bwd = (ncrop - 1) // 2
    split = wrows // 2

    def ring_gather(piece):
        buf = jnp.zeros((ncrop,) + piece.shape, piece.dtype)
        buf = lax.dynamic_update_slice(buf, piece[None], (me, 0, 0))

        fwd = piece
        bwd = piece
        for k in range(1, steps_bwd + 1):
            fwd = lax.ppermute(fwd, "crop", fwd_perm)
            bwd = lax.ppermute(bwd, "crop", bwd_perm)
            buf = lax.dynamic_update_slice(buf, fwd[None], (ring_arr[(pos - k) % ncrop], 0, 0))
            buf = lax.dynamic_update_slice(buf, bwd[None], (ring_arr[(pos + k) % ncrop], 0, 0))
        if steps_fwd > steps_bwd:
            src = ring_arr[(pos - steps_fwd) % ncrop]
            top = lax.ppermute(fwd[:split], "crop", fwd_perm)
            bottom = lax.ppermute(bwd[split:], "crop", bwd_perm)
            buf = lax.dynamic_update_slice(buf, top[None], (src, 0, 0))
            buf = lax.dynamic_update_slice(buf, bottom[None], (src, split, 0))
        return buf.reshape(ncrop * wrows, piece.shape[1])

    kv_weight = ring_gather(jnp.concatenate([key_weight, value_weight], axis=1))
    kv = jnp.dot(tokens_in, kv_weight, preferred_element_type=jnp.float32).astype(jnp.bfloat16)
    packed = kv.reshape(ncrop, CAP, CT, 2 * width)
    incoming = lax.all_to_all(packed, "crop", split_axis=0, concat_axis=0, tiled=True)
    q_weight = ring_gather(query_weight)
    query = jnp.dot(queries_in, q_weight, preferred_element_type=jnp.float32).astype(jnp.bfloat16)
    slotted = incoming.reshape(ncrop * CAP, CT, 2 * width)
    listed = slotted[region_slots].reshape(rows_here, NB * CT, 2 * width)
    keys_row = listed[:, :, :width].reshape(rows_here, NB * CT, heads_here, HD)
    vals_row = listed[:, :, width:].reshape(rows_here, NB * CT, heads_here, HD)
    query_row = query.reshape(rows_here, GR, heads_here, HD)
    scale = 1.0 / HD**0.5
    scores = (
        jnp.einsum("rghe,rkhe->rhgk", query_row, keys_row, preferred_element_type=jnp.float32)
        * scale
    )
    used = (jnp.arange(NB * CT, dtype=jnp.int32) // CT)[None, :] < region_len[:, None]
    scores = jnp.where(used[:, None, None, :], scores, jnp.float32(-1e30))
    top = jnp.max(scores, axis=-1, keepdims=True)
    expo = jnp.exp(scores - top)
    weights = (expo / jnp.sum(expo, axis=-1, keepdims=True)).astype(jnp.bfloat16)
    result = jnp.einsum("rhgk,rkhe->rghe", weights, vals_row, preferred_element_type=jnp.float32)
    return result.astype(jnp.bfloat16).reshape(rows_here * GR, width)


def solution(mesh):
    placed = (
        P("crop", "head"),
        P("crop", "head"),
        P("crop", "head"),
        P("crop", "head"),
        P("crop", "head"),
        P("crop", None, None),
        P("crop", None),
        P("crop"),
    )
    return jax.shard_map(
        body, mesh=mesh, in_specs=placed, out_specs=P("crop", "head"), check_vma=False
    )
```

```python
import jax
import jax.numpy as jnp
from jax import lax
from jax.sharding import PartitionSpec as P

HD = 128
CT = 16
CAP = 2
NB = 8
GR = 32


def ring_order(n):
    half = n // 2
    return [2 * i for i in range(half)] + [2 * i + 1 for i in reversed(range(half))]


def body(
    global_rows,
    crop_tokens,
    query_weight,
    key_weight,
    value_weight,
    fetch_slots,
    region_slots,
    region_len,
):
    width = key_weight.shape[1]
    wrows = key_weight.shape[0]
    heads_here = width // HD
    ncrop = lax.axis_size("crop")
    rows_here = region_slots.shape[0]

    ring = ring_order(ncrop)
    pos_of = [0] * ncrop
    for i, c in enumerate(ring):
        pos_of[c] = i
    me = lax.axis_index("crop")
    pos = jnp.array(pos_of, jnp.int32)[me]
    ring_arr = jnp.array(ring, jnp.int32)
    fwd_perm = [(ring[i], ring[(i + 1) % ncrop]) for i in range(ncrop)]
    bwd_perm = [(ring[i], ring[(i - 1) % ncrop]) for i in range(ncrop)]

    queries_in = lax.all_gather(global_rows, "head", axis=1, tiled=True)
    picks = fetch_slots[0]
    blocks = crop_tokens.reshape(-1, CT, crop_tokens.shape[1])
    chosen = blocks[picks].reshape(-1, crop_tokens.shape[1])
    tokens_in = lax.all_gather(chosen, "head", axis=1, tiled=True)

    steps_fwd = ncrop // 2
    steps_bwd = (ncrop - 1) // 2
    split = wrows // 2

    def ring_gather(piece):
        buf = jnp.zeros((ncrop,) + piece.shape, piece.dtype)
        buf = lax.dynamic_update_slice(buf, piece[None], (me, 0, 0))

        fwd = piece
        bwd = piece
        for k in range(1, steps_bwd + 1):
            fwd = lax.ppermute(fwd, "crop", fwd_perm)
            bwd = lax.ppermute(bwd, "crop", bwd_perm)
            buf = lax.dynamic_update_slice(buf, fwd[None], (ring_arr[(pos - k) % ncrop], 0, 0))
            buf = lax.dynamic_update_slice(buf, bwd[None], (ring_arr[(pos + k) % ncrop], 0, 0))
        if steps_fwd > steps_bwd:
            src = ring_arr[(pos - steps_fwd) % ncrop]
            top = lax.ppermute(fwd[:split], "crop", fwd_perm)
            bottom = lax.ppermute(bwd[split:], "crop", bwd_perm)
            buf = lax.dynamic_update_slice(buf, top[None], (src, 0, 0))
            buf = lax.dynamic_update_slice(buf, bottom[None], (src, split, 0))
        return buf.reshape(ncrop * wrows, piece.shape[1])

    kv_weight = ring_gather(jnp.concatenate([key_weight, value_weight], axis=1))
    kv = jnp.dot(tokens_in, kv_weight, preferred_element_type=jnp.float32).astype(jnp.bfloat16)
    packed = kv.reshape(ncrop, CAP, CT, 2 * width)
    incoming = lax.all_to_all(packed, "crop", split_axis=0, concat_axis=0, tiled=True)
    q_weight = ring_gather(query_weight)
    query = jnp.dot(queries_in, q_weight, preferred_element_type=jnp.float32).astype(jnp.bfloat16)
    nslots = ncrop * CAP
    keys_all = incoming[..., :width].reshape(nslots * CT, heads_here, HD)
    vals_all = incoming[..., width:].reshape(nslots * CT, heads_here, HD)
    query_row = query.reshape(rows_here, GR, heads_here, HD)
    in_use = (jnp.arange(NB, dtype=jnp.int32)[None, :] < region_len[:, None])[:, :, None]
    hits = region_slots[:, :, None] == jnp.arange(nslots, dtype=jnp.int32)[None, None, :]
    member = jnp.any(hits & in_use, axis=1)
    member = jnp.repeat(member, CT, axis=1)
    scale = 1.0 / HD**0.5
    scores = (
        jnp.einsum("rghe,khe->rhgk", query_row, keys_all, preferred_element_type=jnp.float32)
        * scale
    )
    scores = jnp.where(member[:, None, None, :], scores, jnp.float32(-1e30))
    top = jnp.max(scores, axis=-1, keepdims=True)
    expo = jnp.exp(scores - top)
    weights = (expo / jnp.sum(expo, axis=-1, keepdims=True)).astype(jnp.bfloat16)
    result = jnp.einsum("rhgk,khe->rghe", weights, vals_all, preferred_element_type=jnp.float32)
    return result.astype(jnp.bfloat16).reshape(rows_here * GR, width)


def solution(mesh):
    placed = (
        P("crop", "head"),
        P("crop", "head"),
        P("crop", "head"),
        P("crop", "head"),
        P("crop", "head"),
        P("crop", None, None),
        P("crop", None),
        P("crop"),
    )
    return jax.shard_map(
        body, mesh=mesh, in_specs=placed, out_specs=P("crop", "head"), check_vma=False
    )
```

```python
import jax
import jax.numpy as jnp
from jax import lax
from jax.sharding import PartitionSpec as P

HD = 128
CT = 16
CAP = 2
NB = 8
GR = 32


def ring_order(n):
    half = n // 2
    return [2 * i for i in range(half)] + [2 * i + 1 for i in reversed(range(half))]


def body(
    global_rows,
    crop_tokens,
    query_weight,
    key_weight,
    value_weight,
    fetch_slots,
    region_slots,
    region_len,
):
    width = key_weight.shape[1]
    wrows = key_weight.shape[0]
    heads_here = width // HD
    ncrop = lax.axis_size("crop")
    rows_here = region_slots.shape[0]

    ring = ring_order(ncrop)
    pos_of = [0] * ncrop
    for i, c in enumerate(ring):
        pos_of[c] = i
    me = lax.axis_index("crop")
    pos = jnp.array(pos_of, jnp.int32)[me]
    ring_arr = jnp.array(ring, jnp.int32)
    fwd_perm = [(ring[i], ring[(i + 1) % ncrop]) for i in range(ncrop)]
    bwd_perm = [(ring[i], ring[(i - 1) % ncrop]) for i in range(ncrop)]

    queries_in = lax.all_gather(global_rows, "head", axis=1, tiled=True)
    picks = fetch_slots[0]
    blocks = crop_tokens.reshape(-1, CT, crop_tokens.shape[1])
    chosen = blocks[picks].reshape(-1, crop_tokens.shape[1])
    tokens_in = lax.all_gather(chosen, "head", axis=1, tiled=True)

    steps_fwd = ncrop // 2
    steps_bwd = (ncrop - 1) // 2
    split = wrows // 2

    def ring_gather(piece):
        buf = jnp.zeros((ncrop,) + piece.shape, piece.dtype)
        buf = lax.dynamic_update_slice(buf, piece[None], (me, 0, 0))

        fwd = piece
        bwd = piece
        for k in range(1, steps_bwd + 1):
            fwd = lax.ppermute(fwd, "crop", fwd_perm)
            bwd = lax.ppermute(bwd, "crop", bwd_perm)
            buf = lax.dynamic_update_slice(buf, fwd[None], (ring_arr[(pos - k) % ncrop], 0, 0))
            buf = lax.dynamic_update_slice(buf, bwd[None], (ring_arr[(pos + k) % ncrop], 0, 0))
        if steps_fwd > steps_bwd:
            src = ring_arr[(pos - steps_fwd) % ncrop]
            top = lax.ppermute(fwd[:split], "crop", fwd_perm)
            bottom = lax.ppermute(bwd[split:], "crop", bwd_perm)
            buf = lax.dynamic_update_slice(buf, top[None], (src, 0, 0))
            buf = lax.dynamic_update_slice(buf, bottom[None], (src, split, 0))
        return buf.reshape(ncrop * wrows, piece.shape[1])

    kv_weight = ring_gather(jnp.concatenate([key_weight, value_weight], axis=1))
    kv = jnp.dot(tokens_in, kv_weight, preferred_element_type=jnp.float32).astype(jnp.bfloat16)
    packed = kv.reshape(ncrop, CAP, CT, 2 * width)
    incoming = lax.all_to_all(packed, "crop", split_axis=0, concat_axis=0, tiled=True)
    q_piece, kv_weight = lax.optimization_barrier((query_weight, kv_weight))

    def q_part(acc, piece, src, lo, n):
        cols = lax.dynamic_slice_in_dim(queries_in, src * wrows + lo, n, 1)
        return acc + jnp.dot(cols, piece, preferred_element_type=jnp.float32)

    acc = q_part(jnp.zeros((queries_in.shape[0], width), jnp.float32), q_piece, me, 0, wrows)
    fwd = q_piece
    bwd = q_piece
    for k in range(1, steps_bwd + 1):
        fwd = lax.ppermute(fwd, "crop", fwd_perm)
        bwd = lax.ppermute(bwd, "crop", bwd_perm)
        acc = q_part(acc, fwd, ring_arr[(pos - k) % ncrop], 0, wrows)
        acc = q_part(acc, bwd, ring_arr[(pos + k) % ncrop], 0, wrows)
    if steps_fwd > steps_bwd:
        src = ring_arr[(pos - steps_fwd) % ncrop]
        acc = q_part(acc, lax.ppermute(fwd[:split], "crop", fwd_perm), src, 0, split)
        acc = q_part(acc, lax.ppermute(bwd[split:], "crop", bwd_perm), src, split, wrows - split)
    query = acc.astype(jnp.bfloat16)
    nslots = ncrop * CAP
    keys_all = incoming[..., :width].reshape(nslots * CT, heads_here, HD)
    vals_all = incoming[..., width:].reshape(nslots * CT, heads_here, HD)
    query_row = query.reshape(rows_here, GR, heads_here, HD)
    in_use = (jnp.arange(NB, dtype=jnp.int32)[None, :] < region_len[:, None])[:, :, None]
    hits = region_slots[:, :, None] == jnp.arange(nslots, dtype=jnp.int32)[None, None, :]
    member = jnp.any(hits & in_use, axis=1)
    member = jnp.repeat(member, CT, axis=1)
    scale = 1.0 / HD**0.5
    scores = (
        jnp.einsum("rghe,khe->rhgk", query_row, keys_all, preferred_element_type=jnp.float32)
        * scale
    )
    scores = jnp.where(member[:, None, None, :], scores, jnp.float32(-1e30))
    top = jnp.max(scores, axis=-1, keepdims=True)
    expo = jnp.exp(scores - top)
    weights = (expo / jnp.sum(expo, axis=-1, keepdims=True)).astype(jnp.bfloat16)
    result = jnp.einsum("rhgk,khe->rghe", weights, vals_all, preferred_element_type=jnp.float32)
    return result.astype(jnp.bfloat16).reshape(rows_here * GR, width)


def solution(mesh):
    placed = (
        P("crop", "head"),
        P("crop", "head"),
        P("crop", "head"),
        P("crop", "head"),
        P("crop", "head"),
        P("crop", None, None),
        P("crop", None),
        P("crop"),
    )
    return jax.shard_map(
        body, mesh=mesh, in_specs=placed, out_specs=P("crop", "head"), check_vma=False
    )
```

```python
import jax
import jax.numpy as jnp
from jax import lax
from jax.sharding import PartitionSpec as P

HD = 128
CT = 16
CAP = 2
NB = 8
GR = 32


def ring_order(n):
    half = n // 2
    return [2 * i for i in range(half)] + [2 * i + 1 for i in reversed(range(half))]


def body(
    global_rows,
    crop_tokens,
    query_weight,
    key_weight,
    value_weight,
    fetch_slots,
    region_slots,
    region_len,
):
    width = key_weight.shape[1]
    wrows = key_weight.shape[0]
    heads_here = width // HD
    ncrop = lax.axis_size("crop")
    rows_here = region_slots.shape[0]

    ring = ring_order(ncrop)
    pos_of = [0] * ncrop
    for i, c in enumerate(ring):
        pos_of[c] = i
    me = lax.axis_index("crop")
    pos = jnp.array(pos_of, jnp.int32)[me]
    ring_arr = jnp.array(ring, jnp.int32)
    fwd_perm = [(ring[i], ring[(i + 1) % ncrop]) for i in range(ncrop)]
    bwd_perm = [(ring[i], ring[(i - 1) % ncrop]) for i in range(ncrop)]

    queries_in = lax.all_gather(global_rows, "head", axis=1, tiled=True)
    picks = fetch_slots[0]
    blocks = crop_tokens.reshape(-1, CT, crop_tokens.shape[1])
    chosen = blocks[picks]
    delivered = lax.all_to_all(chosen, "crop", split_axis=0, concat_axis=0, tiled=True)
    delivered = delivered.reshape(-1, crop_tokens.shape[1])

    steps_fwd = ncrop // 2
    steps_bwd = (ncrop - 1) // 2
    split = wrows // 2

    def ring_pieces(piece):
        got = [(piece, me, 0, wrows)]
        fwd = piece
        bwd = piece
        for k in range(1, steps_bwd + 1):
            fwd = lax.ppermute(fwd, "crop", fwd_perm)
            bwd = lax.ppermute(bwd, "crop", bwd_perm)
            got.append((fwd, ring_arr[(pos - k) % ncrop], 0, wrows))
            got.append((bwd, ring_arr[(pos + k) % ncrop], 0, wrows))
        if steps_fwd > steps_bwd:
            src = ring_arr[(pos - steps_fwd) % ncrop]
            got.append((lax.ppermute(fwd[:split], "crop", fwd_perm), src, 0, split))
            got.append((lax.ppermute(bwd[split:], "crop", bwd_perm), src, split, wrows - split))
        return got

    kv_got = ring_pieces(jnp.concatenate([key_weight, value_weight], axis=1))
    q_piece, last_a, last_b = lax.optimization_barrier(
        (query_weight, kv_got[-1][0], kv_got[-2][0])
    )
    kv_got[-1] = (last_a,) + kv_got[-1][1:]
    kv_got[-2] = (last_b,) + kv_got[-2][1:]
    tokens_in = lax.all_gather(delivered, "head", axis=1, tiled=True)
    kv_weight = jnp.concatenate([p for p, _, _, _ in kv_got], axis=0)
    tokens_perm = jnp.concatenate(
        [lax.dynamic_slice_in_dim(tokens_in, src * wrows + lo, n, 1) for _, src, lo, n in kv_got],
        axis=1,
    )
    kv = jnp.dot(tokens_perm, kv_weight, preferred_element_type=jnp.float32).astype(jnp.bfloat16)
    incoming = kv.reshape(ncrop, CAP, CT, 2 * width)

    def q_part(acc, piece, src, lo, n):
        cols = lax.dynamic_slice_in_dim(queries_in, src * wrows + lo, n, 1)
        return acc + jnp.dot(cols, piece, preferred_element_type=jnp.float32)

    acc = q_part(jnp.zeros((queries_in.shape[0], width), jnp.float32), q_piece, me, 0, wrows)
    fwd = q_piece
    bwd = q_piece
    for k in range(1, steps_bwd + 1):
        fwd = lax.ppermute(fwd, "crop", fwd_perm)
        bwd = lax.ppermute(bwd, "crop", bwd_perm)
        acc = q_part(acc, fwd, ring_arr[(pos - k) % ncrop], 0, wrows)
        acc = q_part(acc, bwd, ring_arr[(pos + k) % ncrop], 0, wrows)
    if steps_fwd > steps_bwd:
        src = ring_arr[(pos - steps_fwd) % ncrop]
        acc = q_part(acc, lax.ppermute(fwd[:split], "crop", fwd_perm), src, 0, split)
        acc = q_part(acc, lax.ppermute(bwd[split:], "crop", bwd_perm), src, split, wrows - split)
    query = acc.astype(jnp.bfloat16)
    nslots = ncrop * CAP
    keys_all = incoming[..., :width].reshape(nslots * CT, heads_here, HD)
    vals_all = incoming[..., width:].reshape(nslots * CT, heads_here, HD)
    query_row = query.reshape(rows_here, GR, heads_here, HD)
    in_use = (jnp.arange(NB, dtype=jnp.int32)[None, :] < region_len[:, None])[:, :, None]
    hits = region_slots[:, :, None] == jnp.arange(nslots, dtype=jnp.int32)[None, None, :]
    member = jnp.any(hits & in_use, axis=1)
    member = jnp.repeat(member, CT, axis=1)
    scale = 1.0 / HD**0.5
    scores = (
        jnp.einsum("rghe,khe->rhgk", query_row, keys_all, preferred_element_type=jnp.float32)
        * scale
    )
    scores = jnp.where(member[:, None, None, :], scores, jnp.float32(-1e30))
    top = jnp.max(scores, axis=-1, keepdims=True)
    expo = jnp.exp(scores - top)
    weights = (expo / jnp.sum(expo, axis=-1, keepdims=True)).astype(jnp.bfloat16)
    result = jnp.einsum("rhgk,khe->rghe", weights, vals_all, preferred_element_type=jnp.float32)
    return result.astype(jnp.bfloat16).reshape(rows_here * GR, width)


def solution(mesh):
    placed = (
        P("crop", "head"),
        P("crop", "head"),
        P("crop", "head"),
        P("crop", "head"),
        P("crop", "head"),
        P("crop", None, None),
        P("crop", None),
        P("crop"),
    )
    return jax.shard_map(
        body, mesh=mesh, in_specs=placed, out_specs=P("crop", "head"), check_vma=False
    )
```

```python
import jax
import jax.numpy as jnp
from jax import lax
from jax.sharding import PartitionSpec as P

HD = 128
CT = 16
CAP = 2
NB = 8
GR = 32


def ring_order(n):
    half = n // 2
    return [2 * i for i in range(half)] + [2 * i + 1 for i in reversed(range(half))]


def body(
    global_rows,
    crop_tokens,
    query_weight,
    key_weight,
    value_weight,
    fetch_slots,
    region_slots,
    region_len,
):
    width = key_weight.shape[1]
    wrows = key_weight.shape[0]
    heads_here = width // HD
    ncrop = lax.axis_size("crop")
    rows_here = region_slots.shape[0]

    ring = ring_order(ncrop)
    pos_of = [0] * ncrop
    for i, c in enumerate(ring):
        pos_of[c] = i
    me = lax.axis_index("crop")
    pos = jnp.array(pos_of, jnp.int32)[me]
    ring_arr = jnp.array(ring, jnp.int32)
    fwd_perm = [(ring[i], ring[(i + 1) % ncrop]) for i in range(ncrop)]
    bwd_perm = [(ring[i], ring[(i - 1) % ncrop]) for i in range(ncrop)]

    nhead = lax.axis_size("head")
    hme = lax.axis_index("head")

    def head_gather(x):
        full = jnp.zeros((x.shape[0], nhead * x.shape[1]), x.dtype)
        full = lax.dynamic_update_slice(full, x, (0, hme * x.shape[1]))
        for k in range(1, nhead):
            part = lax.ppermute(x, "head", [(j, (j + k) % nhead) for j in range(nhead)])
            full = lax.dynamic_update_slice(full, part, (0, ((hme - k) % nhead) * x.shape[1]))
        return full

    queries_in = head_gather(global_rows)
    picks = fetch_slots[0]
    blocks = crop_tokens.reshape(-1, CT, crop_tokens.shape[1])

    steps_fwd = ncrop // 2
    steps_bwd = (ncrop - 1) // 2
    split = wrows // 2

    def ring_pieces(pieces):
        got = [[(p, me, 0, wrows)] for p in pieces]
        fwd = list(pieces)
        bwd = list(pieces)
        for k in range(1, steps_bwd + 1):
            for i in range(len(pieces)):
                fwd[i] = lax.ppermute(fwd[i], "crop", fwd_perm)
                bwd[i] = lax.ppermute(bwd[i], "crop", bwd_perm)
                got[i].append((fwd[i], ring_arr[(pos - k) % ncrop], 0, wrows))
                got[i].append((bwd[i], ring_arr[(pos + k) % ncrop], 0, wrows))
        if steps_fwd > steps_bwd:
            src = ring_arr[(pos - steps_fwd) % ncrop]
            for i in range(len(pieces)):
                top = lax.ppermute(fwd[i][:split], "crop", fwd_perm)
                bottom = lax.ppermute(bwd[i][split:], "crop", bwd_perm)
                got[i].append((top, src, 0, split))
                got[i].append((bottom, src, split, wrows - split))
        return got

    k_got, v_got = ring_pieces([key_weight, value_weight])
    chosen, k_first, v_first = lax.optimization_barrier((blocks[picks], k_got[1][0], v_got[1][0]))
    k_got[1] = (k_first,) + k_got[1][1:]
    v_got[1] = (v_first,) + v_got[1][1:]
    delivered = lax.all_to_all(chosen, "crop", split_axis=0, concat_axis=0, tiled=True)
    tokens_in = head_gather(delivered.reshape(-1, crop_tokens.shape[1]))
    q_piece, k_last, v_last = lax.optimization_barrier((query_weight, k_got[-1][0], v_got[-1][0]))
    k_got[-1] = (k_last,) + k_got[-1][1:]
    v_got[-1] = (v_last,) + v_got[-1][1:]
    tokens_perm = jnp.concatenate(
        [lax.dynamic_slice_in_dim(tokens_in, src * wrows + lo, n, 1) for _, src, lo, n in k_got],
        axis=1,
    )

    def project(got):
        weight = jnp.concatenate([p for p, _, _, _ in got], axis=0)
        out = jnp.dot(tokens_perm, weight, preferred_element_type=jnp.float32)
        return out.astype(jnp.bfloat16)

    keys_all = project(k_got)
    vals_all = project(v_got)

    def q_part(acc, piece, src, lo, n):
        cols = lax.dynamic_slice_in_dim(queries_in, src * wrows + lo, n, 1)
        return acc + jnp.dot(cols, piece, preferred_element_type=jnp.float32)

    acc = q_part(jnp.zeros((queries_in.shape[0], width), jnp.float32), q_piece, me, 0, wrows)
    fwd = q_piece
    bwd = q_piece
    for k in range(1, steps_bwd + 1):
        fwd = lax.ppermute(fwd, "crop", fwd_perm)
        bwd = lax.ppermute(bwd, "crop", bwd_perm)
        acc = q_part(acc, fwd, ring_arr[(pos - k) % ncrop], 0, wrows)
        acc = q_part(acc, bwd, ring_arr[(pos + k) % ncrop], 0, wrows)
    if steps_fwd > steps_bwd:
        src = ring_arr[(pos - steps_fwd) % ncrop]
        acc = q_part(acc, lax.ppermute(fwd[:split], "crop", fwd_perm), src, 0, split)
        acc = q_part(acc, lax.ppermute(bwd[split:], "crop", bwd_perm), src, split, wrows - split)
    query = acc.astype(jnp.bfloat16)
    nslots = ncrop * CAP
    keys_all = keys_all.reshape(nslots * CT, heads_here, HD)
    vals_all = vals_all.reshape(nslots * CT, heads_here, HD)
    query_row = query.reshape(rows_here, GR, heads_here, HD)
    in_use = (jnp.arange(NB, dtype=jnp.int32)[None, :] < region_len[:, None])[:, :, None]
    hits = region_slots[:, :, None] == jnp.arange(nslots, dtype=jnp.int32)[None, None, :]
    member = jnp.any(hits & in_use, axis=1)
    member = jnp.repeat(member, CT, axis=1)
    scale = 1.0 / HD**0.5
    scores = (
        jnp.einsum("rghe,khe->rhgk", query_row, keys_all, preferred_element_type=jnp.float32)
        * scale
    )
    scores = jnp.where(member[:, None, None, :], scores, jnp.float32(-1e30))
    top = jnp.max(scores, axis=-1, keepdims=True)
    expo = jnp.exp(scores - top)
    weights = (expo / jnp.sum(expo, axis=-1, keepdims=True)).astype(jnp.bfloat16)
    result = jnp.einsum("rhgk,khe->rghe", weights, vals_all, preferred_element_type=jnp.float32)
    return result.astype(jnp.bfloat16).reshape(rows_here * GR, width)


def solution(mesh):
    placed = (
        P("crop", "head"),
        P("crop", "head"),
        P("crop", "head"),
        P("crop", "head"),
        P("crop", "head"),
        P("crop", None, None),
        P("crop", None),
        P("crop"),
    )
    return jax.shard_map(
        body, mesh=mesh, in_specs=placed, out_specs=P("crop", "head"), check_vma=False
    )
```

```python
import jax
import jax.numpy as jnp
from jax import lax
from jax.sharding import PartitionSpec as P

HD = 128
CT = 16
CAP = 2
NB = 8
GR = 32


def ring_order(n):
    half = n // 2
    return [2 * i for i in range(half)] + [2 * i + 1 for i in reversed(range(half))]


def body(
    global_rows,
    crop_tokens,
    query_weight,
    key_weight,
    value_weight,
    fetch_slots,
    region_slots,
    region_len,
):
    width = key_weight.shape[1]
    wrows = key_weight.shape[0]
    heads_here = width // HD
    ncrop = lax.axis_size("crop")
    rows_here = region_slots.shape[0]

    ring = ring_order(ncrop)
    pos_of = [0] * ncrop
    for i, c in enumerate(ring):
        pos_of[c] = i
    me = lax.axis_index("crop")
    pos = jnp.array(pos_of, jnp.int32)[me]
    ring_arr = jnp.array(ring, jnp.int32)
    fwd_perm = [(ring[i], ring[(i + 1) % ncrop]) for i in range(ncrop)]
    bwd_perm = [(ring[i], ring[(i - 1) % ncrop]) for i in range(ncrop)]

    queries_in = lax.all_gather(global_rows, "head", axis=1, tiled=True)
    picks = fetch_slots[0]
    blocks = crop_tokens.reshape(-1, CT, crop_tokens.shape[1])

    steps_fwd = ncrop // 2
    steps_bwd = (ncrop - 1) // 2
    split = wrows // 2

    def ring_pieces(piece):
        got = [(piece, me, 0, wrows)]
        fwd = piece
        bwd = piece
        for k in range(1, steps_bwd + 1):
            fwd = lax.ppermute(fwd, "crop", fwd_perm)
            bwd = lax.ppermute(bwd, "crop", bwd_perm)
            got.append((fwd, ring_arr[(pos - k) % ncrop], 0, wrows))
            got.append((bwd, ring_arr[(pos + k) % ncrop], 0, wrows))
        if steps_fwd > steps_bwd:
            src = ring_arr[(pos - steps_fwd) % ncrop]
            got.append((lax.ppermute(fwd[:split], "crop", fwd_perm), src, 0, split))
            got.append((lax.ppermute(bwd[split:], "crop", bwd_perm), src, split, wrows - split))
        return got

    kv_got = ring_pieces(jnp.concatenate([key_weight, value_weight], axis=1))
    q_piece, last_a, last_b = lax.optimization_barrier(
        (query_weight, kv_got[-1][0], kv_got[-2][0])
    )
    kv_got[-1] = (last_a,) + kv_got[-1][1:]
    kv_got[-2] = (last_b,) + kv_got[-2][1:]
    chosen, first = lax.optimization_barrier((blocks[picks], kv_got[1][0]))
    kv_got[1] = (first,) + kv_got[1][1:]
    delivered = lax.all_to_all(chosen, "crop", split_axis=0, concat_axis=0, tiled=True)
    delivered = delivered.reshape(-1, crop_tokens.shape[1])
    tokens_in = lax.all_gather(delivered, "head", axis=1, tiled=True)
    kv_weight = jnp.concatenate([p for p, _, _, _ in kv_got], axis=0)
    tokens_perm = jnp.concatenate(
        [lax.dynamic_slice_in_dim(tokens_in, src * wrows + lo, n, 1) for _, src, lo, n in kv_got],
        axis=1,
    )
    kv = jnp.dot(tokens_perm, kv_weight, preferred_element_type=jnp.float32).astype(jnp.bfloat16)
    incoming = kv.reshape(ncrop, CAP, CT, 2 * width)

    def q_part(acc, piece, src, lo, n):
        cols = lax.dynamic_slice_in_dim(queries_in, src * wrows + lo, n, 1)
        return acc + jnp.dot(cols, piece, preferred_element_type=jnp.float32)

    acc = q_part(jnp.zeros((queries_in.shape[0], width), jnp.float32), q_piece, me, 0, wrows)
    fwd = q_piece
    bwd = q_piece
    for k in range(1, steps_bwd + 1):
        fwd = lax.ppermute(fwd, "crop", fwd_perm)
        bwd = lax.ppermute(bwd, "crop", bwd_perm)
        acc = q_part(acc, fwd, ring_arr[(pos - k) % ncrop], 0, wrows)
        acc = q_part(acc, bwd, ring_arr[(pos + k) % ncrop], 0, wrows)
    if steps_fwd > steps_bwd:
        src = ring_arr[(pos - steps_fwd) % ncrop]
        acc = q_part(acc, lax.ppermute(fwd[:split], "crop", fwd_perm), src, 0, split)
        acc = q_part(acc, lax.ppermute(bwd[split:], "crop", bwd_perm), src, split, wrows - split)
    query = acc.astype(jnp.bfloat16)
    nslots = ncrop * CAP
    keys_all = incoming[..., :width].reshape(nslots * CT, heads_here, HD)
    vals_all = incoming[..., width:].reshape(nslots * CT, heads_here, HD)
    query_row = query.reshape(rows_here, GR, heads_here, HD)
    in_use = (jnp.arange(NB, dtype=jnp.int32)[None, :] < region_len[:, None])[:, :, None]
    hits = region_slots[:, :, None] == jnp.arange(nslots, dtype=jnp.int32)[None, None, :]
    member = jnp.any(hits & in_use, axis=1)
    member = jnp.repeat(member, CT, axis=1)
    scale = 1.0 / HD**0.5
    scores = (
        jnp.einsum("rghe,khe->rhgk", query_row, keys_all, preferred_element_type=jnp.float32)
        * scale
    )
    scores = jnp.where(member[:, None, None, :], scores, jnp.float32(-1e30))
    top = jnp.max(scores, axis=-1, keepdims=True)
    expo = jnp.exp(scores - top)
    weights = (expo / jnp.sum(expo, axis=-1, keepdims=True)).astype(jnp.bfloat16)
    result = jnp.einsum("rhgk,khe->rghe", weights, vals_all, preferred_element_type=jnp.float32)
    return result.astype(jnp.bfloat16).reshape(rows_here * GR, width)


def solution(mesh):
    placed = (
        P("crop", "head"),
        P("crop", "head"),
        P("crop", "head"),
        P("crop", "head"),
        P("crop", "head"),
        P("crop", None, None),
        P("crop", None),
        P("crop"),
    )
    return jax.shard_map(
        body, mesh=mesh, in_specs=placed, out_specs=P("crop", "head"), check_vma=False
    )
```

```python
import jax
import jax.numpy as jnp
from jax import lax
from jax.sharding import PartitionSpec as P

HD = 128
CT = 16
CAP = 2
NB = 8
GR = 32


def ring_order(n):
    half = n // 2
    return [2 * i for i in range(half)] + [2 * i + 1 for i in reversed(range(half))]


def body(
    global_rows,
    crop_tokens,
    query_weight,
    key_weight,
    value_weight,
    fetch_slots,
    region_slots,
    region_len,
):
    width = key_weight.shape[1]
    wrows = key_weight.shape[0]
    heads_here = width // HD
    ncrop = lax.axis_size("crop")
    rows_here = region_slots.shape[0]

    ring = ring_order(ncrop)
    pos_of = [0] * ncrop
    for i, c in enumerate(ring):
        pos_of[c] = i
    me = lax.axis_index("crop")
    pos = jnp.array(pos_of, jnp.int32)[me]
    ring_arr = jnp.array(ring, jnp.int32)
    fwd_perm = [(ring[i], ring[(i + 1) % ncrop]) for i in range(ncrop)]
    bwd_perm = [(ring[i], ring[(i - 1) % ncrop]) for i in range(ncrop)]

    nhead = lax.axis_size("head")
    hme = lax.axis_index("head")

    def head_gather(x):
        full = jnp.zeros((x.shape[0], nhead * x.shape[1]), x.dtype)
        full = lax.dynamic_update_slice(full, x, (0, hme * x.shape[1]))
        for k in range(1, nhead):
            part = lax.ppermute(x, "head", [(j, (j + k) % nhead) for j in range(nhead)])
            full = lax.dynamic_update_slice(full, part, (0, ((hme - k) % nhead) * x.shape[1]))
        return full

    queries_in = head_gather(global_rows)
    picks = fetch_slots[0]
    blocks = crop_tokens.reshape(-1, CT, crop_tokens.shape[1])
    chosen = blocks[picks]
    delivered = lax.all_to_all(chosen, "crop", split_axis=0, concat_axis=0, tiled=True)
    delivered = delivered.reshape(-1, crop_tokens.shape[1])

    steps_fwd = ncrop // 2
    steps_bwd = (ncrop - 1) // 2
    split = wrows // 2

    def ring_pieces(piece):
        got = [(piece, me, 0, wrows)]
        fwd = piece
        bwd = piece
        for k in range(1, steps_bwd + 1):
            fwd = lax.ppermute(fwd, "crop", fwd_perm)
            bwd = lax.ppermute(bwd, "crop", bwd_perm)
            got.append((fwd, ring_arr[(pos - k) % ncrop], 0, wrows))
            got.append((bwd, ring_arr[(pos + k) % ncrop], 0, wrows))
        if steps_fwd > steps_bwd:
            src = ring_arr[(pos - steps_fwd) % ncrop]
            got.append((lax.ppermute(fwd[:split], "crop", fwd_perm), src, 0, split))
            got.append((lax.ppermute(bwd[split:], "crop", bwd_perm), src, split, wrows - split))
        return got

    kv_got = ring_pieces(jnp.concatenate([key_weight, value_weight], axis=1))
    q_piece, last_a, last_b = lax.optimization_barrier(
        (query_weight, kv_got[-1][0], kv_got[-2][0])
    )
    kv_got[-1] = (last_a,) + kv_got[-1][1:]
    kv_got[-2] = (last_b,) + kv_got[-2][1:]
    tokens_in = head_gather(delivered)
    kv_weight = jnp.concatenate([p for p, _, _, _ in kv_got], axis=0)
    tokens_perm = jnp.concatenate(
        [lax.dynamic_slice_in_dim(tokens_in, src * wrows + lo, n, 1) for _, src, lo, n in kv_got],
        axis=1,
    )
    kv = jnp.dot(tokens_perm, kv_weight, preferred_element_type=jnp.float32).astype(jnp.bfloat16)
    incoming = kv.reshape(ncrop, CAP, CT, 2 * width)

    def q_part(acc, piece, src, lo, n):
        cols = lax.dynamic_slice_in_dim(queries_in, src * wrows + lo, n, 1)
        return acc + jnp.dot(cols, piece, preferred_element_type=jnp.float32)

    acc = q_part(jnp.zeros((queries_in.shape[0], width), jnp.float32), q_piece, me, 0, wrows)
    fwd = q_piece
    bwd = q_piece
    for k in range(1, steps_bwd + 1):
        fwd = lax.ppermute(fwd, "crop", fwd_perm)
        bwd = lax.ppermute(bwd, "crop", bwd_perm)
        acc = q_part(acc, fwd, ring_arr[(pos - k) % ncrop], 0, wrows)
        acc = q_part(acc, bwd, ring_arr[(pos + k) % ncrop], 0, wrows)
    if steps_fwd > steps_bwd:
        src = ring_arr[(pos - steps_fwd) % ncrop]
        acc = q_part(acc, lax.ppermute(fwd[:split], "crop", fwd_perm), src, 0, split)
        acc = q_part(acc, lax.ppermute(bwd[split:], "crop", bwd_perm), src, split, wrows - split)
    query = acc.astype(jnp.bfloat16)
    nslots = ncrop * CAP
    keys_all = incoming[..., :width].reshape(nslots * CT, heads_here, HD)
    vals_all = incoming[..., width:].reshape(nslots * CT, heads_here, HD)
    query_row = query.reshape(rows_here, GR, heads_here, HD)
    in_use = (jnp.arange(NB, dtype=jnp.int32)[None, :] < region_len[:, None])[:, :, None]
    hits = region_slots[:, :, None] == jnp.arange(nslots, dtype=jnp.int32)[None, None, :]
    member = jnp.any(hits & in_use, axis=1)
    member = jnp.repeat(member, CT, axis=1)
    scale = 1.0 / HD**0.5
    scores = (
        jnp.einsum("rghe,khe->rhgk", query_row, keys_all, preferred_element_type=jnp.float32)
        * scale
    )
    scores = jnp.where(member[:, None, None, :], scores, jnp.float32(-1e30))
    top = jnp.max(scores, axis=-1, keepdims=True)
    expo = jnp.exp(scores - top)
    weights = (expo / jnp.sum(expo, axis=-1, keepdims=True)).astype(jnp.bfloat16)
    result = jnp.einsum("rhgk,khe->rghe", weights, vals_all, preferred_element_type=jnp.float32)
    return result.astype(jnp.bfloat16).reshape(rows_here * GR, width)


def solution(mesh):
    placed = (
        P("crop", "head"),
        P("crop", "head"),
        P("crop", "head"),
        P("crop", "head"),
        P("crop", "head"),
        P("crop", None, None),
        P("crop", None),
        P("crop"),
    )
    return jax.shard_map(
        body, mesh=mesh, in_specs=placed, out_specs=P("crop", "head"), check_vma=False
    )
```

```python
import jax
import jax.numpy as jnp
from jax import lax
from jax.sharding import PartitionSpec as P

HD = 128
CT = 16
CAP = 2
NB = 8
GR = 32


def ring_order(n):
    half = n // 2
    return [2 * i for i in range(half)] + [2 * i + 1 for i in reversed(range(half))]


def body(
    global_rows,
    crop_tokens,
    query_weight,
    key_weight,
    value_weight,
    fetch_slots,
    region_slots,
    region_len,
):
    width = key_weight.shape[1]
    wrows = key_weight.shape[0]
    heads_here = width // HD
    ncrop = lax.axis_size("crop")
    rows_here = region_slots.shape[0]

    ring = ring_order(ncrop)
    pos_of = [0] * ncrop
    for i, c in enumerate(ring):
        pos_of[c] = i
    me = lax.axis_index("crop")
    pos = jnp.array(pos_of, jnp.int32)[me]
    ring_arr = jnp.array(ring, jnp.int32)
    fwd_perm = [(ring[i], ring[(i + 1) % ncrop]) for i in range(ncrop)]
    bwd_perm = [(ring[i], ring[(i - 1) % ncrop]) for i in range(ncrop)]

    nhead = lax.axis_size("head")
    hme = lax.axis_index("head")

    def head_gather(x):
        full = jnp.zeros((x.shape[0], nhead * x.shape[1]), x.dtype)
        full = lax.dynamic_update_slice(full, x, (0, hme * x.shape[1]))
        for k in range(1, nhead):
            part = lax.ppermute(x, "head", [(j, (j + k) % nhead) for j in range(nhead)])
            full = lax.dynamic_update_slice(full, part, (0, ((hme - k) % nhead) * x.shape[1]))
        return full

    queries_in = head_gather(global_rows)
    picks = fetch_slots[0]
    blocks = crop_tokens.reshape(-1, CT, crop_tokens.shape[1])
    nslots = ncrop * CAP

    steps_fwd = ncrop // 2
    steps_bwd = (ncrop - 1) // 2
    split = wrows // 2

    def q_part(acc, piece, src, lo, n):
        cols = lax.dynamic_slice_in_dim(queries_in, src * wrows + lo, n, 1)
        return acc + jnp.dot(cols, piece, preferred_element_type=jnp.float32)

    acc = q_part(jnp.zeros((queries_in.shape[0], width), jnp.float32), query_weight, me, 0, wrows)
    fwd = query_weight
    bwd = query_weight
    for k in range(1, steps_bwd + 1):
        fwd = lax.ppermute(fwd, "crop", fwd_perm)
        bwd = lax.ppermute(bwd, "crop", bwd_perm)
        acc = q_part(acc, fwd, ring_arr[(pos - k) % ncrop], 0, wrows)
        acc = q_part(acc, bwd, ring_arr[(pos + k) % ncrop], 0, wrows)
    if steps_fwd > steps_bwd:
        src = ring_arr[(pos - steps_fwd) % ncrop]
        acc = q_part(acc, lax.ppermute(fwd[:split], "crop", fwd_perm), src, 0, split)
        acc = q_part(acc, lax.ppermute(bwd[split:], "crop", bwd_perm), src, split, wrows - split)

    chosen = blocks[picks].reshape(-1, crop_tokens.shape[1])
    chosen_full = head_gather(chosen)
    sent = chosen_full.reshape(chosen_full.shape[0], ncrop, wrows).transpose(1, 0, 2)
    got = lax.all_to_all(sent, "crop", split_axis=0, concat_axis=0, tiled=True)
    got = got.reshape(ncrop, ncrop, CAP * CT, wrows).transpose(1, 0, 2, 3)
    own_cols = got.reshape(ncrop, nslots * CT, wrows)

    def partial(dest, weight):
        rows = lax.dynamic_index_in_dim(own_cols, dest, 0, keepdims=False)
        return jnp.dot(rows, weight, preferred_element_type=jnp.float32)

    def reduce_ring(weight, perm, step):
        if ncrop == 1:
            return partial(me, weight).astype(jnp.bfloat16)
        send = partial(ring_arr[(pos + step) % ncrop], weight).astype(jnp.bfloat16)
        for k in range(1, ncrop):
            recv = lax.ppermute(send, "crop", perm).astype(jnp.float32)
            if k < ncrop - 1:
                nxt = ring_arr[(pos + step * (k + 1)) % ncrop]
                send = (recv + partial(nxt, weight)).astype(jnp.bfloat16)
            else:
                return (recv + partial(me, weight)).astype(jnp.bfloat16)

    keys_all = reduce_ring(key_weight, fwd_perm, -1)
    vals_all = reduce_ring(value_weight, bwd_perm, 1)
    query = acc.astype(jnp.bfloat16)
    nslots = ncrop * CAP
    keys_all = keys_all.reshape(nslots * CT, heads_here, HD)
    vals_all = vals_all.reshape(nslots * CT, heads_here, HD)
    query_row = query.reshape(rows_here, GR, heads_here, HD)
    in_use = (jnp.arange(NB, dtype=jnp.int32)[None, :] < region_len[:, None])[:, :, None]
    hits = region_slots[:, :, None] == jnp.arange(nslots, dtype=jnp.int32)[None, None, :]
    member = jnp.any(hits & in_use, axis=1)
    member = jnp.repeat(member, CT, axis=1)
    scale = 1.0 / HD**0.5
    scores = (
        jnp.einsum("rghe,khe->rhgk", query_row, keys_all, preferred_element_type=jnp.float32)
        * scale
    )
    scores = jnp.where(member[:, None, None, :], scores, jnp.float32(-1e30))
    top = jnp.max(scores, axis=-1, keepdims=True)
    expo = jnp.exp(scores - top)
    weights = (expo / jnp.sum(expo, axis=-1, keepdims=True)).astype(jnp.bfloat16)
    result = jnp.einsum("rhgk,khe->rghe", weights, vals_all, preferred_element_type=jnp.float32)
    return result.astype(jnp.bfloat16).reshape(rows_here * GR, width)


def solution(mesh):
    placed = (
        P("crop", "head"),
        P("crop", "head"),
        P("crop", "head"),
        P("crop", "head"),
        P("crop", "head"),
        P("crop", None, None),
        P("crop", None),
        P("crop"),
    )
    return jax.shard_map(
        body, mesh=mesh, in_specs=placed, out_specs=P("crop", "head"), check_vma=False
    )
```

```python
import jax
import jax.numpy as jnp
from jax import lax
from jax.sharding import PartitionSpec as P

HD = 128
CT = 16
CAP = 2
NB = 8
GR = 32


def ring_order(n):
    half = n // 2
    return [2 * i for i in range(half)] + [2 * i + 1 for i in reversed(range(half))]


def body(
    global_rows,
    crop_tokens,
    query_weight,
    key_weight,
    value_weight,
    fetch_slots,
    region_slots,
    region_len,
):
    width = key_weight.shape[1]
    wrows = key_weight.shape[0]
    heads_here = width // HD
    ncrop = lax.axis_size("crop")
    rows_here = region_slots.shape[0]

    ring = ring_order(ncrop)
    pos_of = [0] * ncrop
    for i, c in enumerate(ring):
        pos_of[c] = i
    me = lax.axis_index("crop")
    pos = jnp.array(pos_of, jnp.int32)[me]
    ring_arr = jnp.array(ring, jnp.int32)
    fwd_perm = [(ring[i], ring[(i + 1) % ncrop]) for i in range(ncrop)]
    bwd_perm = [(ring[i], ring[(i - 1) % ncrop]) for i in range(ncrop)]

    nhead = lax.axis_size("head")
    hme = lax.axis_index("head")

    def head_gather(x):
        full = jnp.zeros((x.shape[0], nhead * x.shape[1]), x.dtype)
        full = lax.dynamic_update_slice(full, x, (0, hme * x.shape[1]))
        for k in range(1, nhead):
            part = lax.ppermute(x, "head", [(j, (j + k) % nhead) for j in range(nhead)])
            full = lax.dynamic_update_slice(full, part, (0, ((hme - k) % nhead) * x.shape[1]))
        return full

    queries_in = head_gather(global_rows)
    picks = fetch_slots[0]
    blocks = crop_tokens.reshape(-1, CT, crop_tokens.shape[1])
    nslots = ncrop * CAP

    steps_fwd = ncrop // 2
    steps_bwd = (ncrop - 1) // 2
    split = wrows // 2

    chosen = blocks[picks].reshape(-1, crop_tokens.shape[1])
    chosen_full = head_gather(chosen)
    sent = chosen_full.reshape(chosen_full.shape[0], ncrop, wrows).transpose(1, 0, 2)
    got = lax.all_to_all(sent, "crop", split_axis=0, concat_axis=0, tiled=True)
    got = got.reshape(ncrop, ncrop, CAP * CT, wrows).transpose(1, 0, 2, 3)
    own_cols = got.reshape(ncrop, nslots * CT, wrows)

    def q_part(acc, piece, src, lo, n):
        cols = lax.dynamic_slice_in_dim(queries_in, src * wrows + lo, n, 1)
        return acc + jnp.dot(cols, piece, preferred_element_type=jnp.float32)

    q_piece, own_cols = lax.optimization_barrier((query_weight, own_cols))
    acc = q_part(jnp.zeros((queries_in.shape[0], width), jnp.float32), q_piece, me, 0, wrows)
    fwd = q_piece
    bwd = q_piece
    for k in range(1, steps_bwd + 1):
        fwd = lax.ppermute(fwd, "crop", fwd_perm)
        bwd = lax.ppermute(bwd, "crop", bwd_perm)
        acc = q_part(acc, fwd, ring_arr[(pos - k) % ncrop], 0, wrows)
        acc = q_part(acc, bwd, ring_arr[(pos + k) % ncrop], 0, wrows)
    if steps_fwd > steps_bwd:
        src = ring_arr[(pos - steps_fwd) % ncrop]
        acc = q_part(acc, lax.ppermute(fwd[:split], "crop", fwd_perm), src, 0, split)
        acc = q_part(acc, lax.ppermute(bwd[split:], "crop", bwd_perm), src, split, wrows - split)

    def partial(dest, weight):
        rows = lax.dynamic_index_in_dim(own_cols, dest, 0, keepdims=False)
        return jnp.dot(rows, weight, preferred_element_type=jnp.float32)

    def reduce_ring(weight, perm, step):
        if ncrop == 1:
            return partial(me, weight).astype(jnp.bfloat16)
        send = partial(ring_arr[(pos + step) % ncrop], weight).astype(jnp.bfloat16)
        for k in range(1, ncrop):
            recv = lax.ppermute(send, "crop", perm).astype(jnp.float32)
            if k < ncrop - 1:
                nxt = ring_arr[(pos + step * (k + 1)) % ncrop]
                send = (recv + partial(nxt, weight)).astype(jnp.bfloat16)
            else:
                return (recv + partial(me, weight)).astype(jnp.bfloat16)

    keys_all = reduce_ring(key_weight, fwd_perm, -1)
    vals_all = reduce_ring(value_weight, bwd_perm, 1)
    query = acc.astype(jnp.bfloat16)
    nslots = ncrop * CAP
    keys_all = keys_all.reshape(nslots * CT, heads_here, HD)
    vals_all = vals_all.reshape(nslots * CT, heads_here, HD)
    query_row = query.reshape(rows_here, GR, heads_here, HD)
    in_use = (jnp.arange(NB, dtype=jnp.int32)[None, :] < region_len[:, None])[:, :, None]
    hits = region_slots[:, :, None] == jnp.arange(nslots, dtype=jnp.int32)[None, None, :]
    member = jnp.any(hits & in_use, axis=1)
    member = jnp.repeat(member, CT, axis=1)
    scale = 1.0 / HD**0.5
    scores = (
        jnp.einsum("rghe,khe->rhgk", query_row, keys_all, preferred_element_type=jnp.float32)
        * scale
    )
    scores = jnp.where(member[:, None, None, :], scores, jnp.float32(-1e30))
    top = jnp.max(scores, axis=-1, keepdims=True)
    expo = jnp.exp(scores - top)
    weights = (expo / jnp.sum(expo, axis=-1, keepdims=True)).astype(jnp.bfloat16)
    result = jnp.einsum("rhgk,khe->rghe", weights, vals_all, preferred_element_type=jnp.float32)
    return result.astype(jnp.bfloat16).reshape(rows_here * GR, width)


def solution(mesh):
    placed = (
        P("crop", "head"),
        P("crop", "head"),
        P("crop", "head"),
        P("crop", "head"),
        P("crop", "head"),
        P("crop", None, None),
        P("crop", None),
        P("crop"),
    )
    return jax.shard_map(
        body, mesh=mesh, in_specs=placed, out_specs=P("crop", "head"), check_vma=False
    )
```

```python
import jax
import jax.numpy as jnp
from jax import lax
from jax.sharding import PartitionSpec as P

HD = 128
CT = 16
CAP = 2
NB = 8
GR = 32


def ring_order(n):
    half = n // 2
    return [2 * i for i in range(half)] + [2 * i + 1 for i in reversed(range(half))]


def body(
    global_rows,
    crop_tokens,
    query_weight,
    key_weight,
    value_weight,
    fetch_slots,
    region_slots,
    region_len,
):
    width = key_weight.shape[1]
    wrows = key_weight.shape[0]
    heads_here = width // HD
    ncrop = lax.axis_size("crop")
    rows_here = region_slots.shape[0]

    ring = ring_order(ncrop)
    pos_of = [0] * ncrop
    for i, c in enumerate(ring):
        pos_of[c] = i
    me = lax.axis_index("crop")
    pos = jnp.array(pos_of, jnp.int32)[me]
    ring_arr = jnp.array(ring, jnp.int32)
    fwd_perm = [(ring[i], ring[(i + 1) % ncrop]) for i in range(ncrop)]
    bwd_perm = [(ring[i], ring[(i - 1) % ncrop]) for i in range(ncrop)]

    nhead = lax.axis_size("head")
    hme = lax.axis_index("head")

    def head_gather(x):
        full = jnp.zeros((x.shape[0], nhead * x.shape[1]), x.dtype)
        full = lax.dynamic_update_slice(full, x, (0, hme * x.shape[1]))
        for k in range(1, nhead):
            part = lax.ppermute(x, "head", [(j, (j + k) % nhead) for j in range(nhead)])
            full = lax.dynamic_update_slice(full, part, (0, ((hme - k) % nhead) * x.shape[1]))
        return full

    queries_in = head_gather(global_rows)
    picks = fetch_slots[0]
    blocks = crop_tokens.reshape(-1, CT, crop_tokens.shape[1])
    chosen = blocks[picks]
    delivered = lax.all_to_all(chosen, "crop", split_axis=0, concat_axis=0, tiled=True)
    delivered = delivered.reshape(-1, crop_tokens.shape[1])

    steps_fwd = ncrop // 2
    steps_bwd = (ncrop - 1) // 2
    split = wrows // 2

    def ring_pieces(piece):
        got = [(piece, me, 0, wrows)]
        fwd = piece
        bwd = piece
        half = lambda x, sl: jax.tree.map(lambda a: a[sl], x)
        for k in range(1, steps_bwd + 1):
            fwd = lax.ppermute(fwd, "crop", fwd_perm)
            bwd = lax.ppermute(bwd, "crop", bwd_perm)
            got.append((fwd, ring_arr[(pos - k) % ncrop], 0, wrows))
            got.append((bwd, ring_arr[(pos + k) % ncrop], 0, wrows))
        if steps_fwd > steps_bwd:
            src = ring_arr[(pos - steps_fwd) % ncrop]
            top = lax.ppermute(half(fwd, slice(None, split)), "crop", fwd_perm)
            bottom = lax.ppermute(half(bwd, slice(split, None)), "crop", bwd_perm)
            got.append((top, src, 0, split))
            got.append((bottom, src, split, wrows - split))
        return got

    kv_got = ring_pieces((key_weight, value_weight))
    q_piece, last_a, last_b = lax.optimization_barrier(
        (query_weight, kv_got[-1][0], kv_got[-2][0])
    )
    kv_got[-1] = (last_a,) + kv_got[-1][1:]
    kv_got[-2] = (last_b,) + kv_got[-2][1:]
    tokens_in = head_gather(delivered)
    k_weight = jnp.concatenate([p[0] for p, _, _, _ in kv_got], axis=0)
    v_weight = jnp.concatenate([p[1] for p, _, _, _ in kv_got], axis=0)
    tokens_perm = jnp.concatenate(
        [lax.dynamic_slice_in_dim(tokens_in, src * wrows + lo, n, 1) for _, src, lo, n in kv_got],
        axis=1,
    )
    keys_all = jnp.dot(tokens_perm, k_weight, preferred_element_type=jnp.float32)
    vals_all = jnp.dot(tokens_perm, v_weight, preferred_element_type=jnp.float32)
    keys_all = keys_all.astype(jnp.bfloat16)
    vals_all = vals_all.astype(jnp.bfloat16)

    def q_part(acc, piece, src, lo, n):
        cols = lax.dynamic_slice_in_dim(queries_in, src * wrows + lo, n, 1)
        return acc + jnp.dot(cols, piece, preferred_element_type=jnp.float32)

    acc = q_part(jnp.zeros((queries_in.shape[0], width), jnp.float32), q_piece, me, 0, wrows)
    fwd = q_piece
    bwd = q_piece
    for k in range(1, steps_bwd + 1):
        fwd = lax.ppermute(fwd, "crop", fwd_perm)
        bwd = lax.ppermute(bwd, "crop", bwd_perm)
        acc = q_part(acc, fwd, ring_arr[(pos - k) % ncrop], 0, wrows)
        acc = q_part(acc, bwd, ring_arr[(pos + k) % ncrop], 0, wrows)
    if steps_fwd > steps_bwd:
        src = ring_arr[(pos - steps_fwd) % ncrop]
        acc = q_part(acc, lax.ppermute(fwd[:split], "crop", fwd_perm), src, 0, split)
        acc = q_part(acc, lax.ppermute(bwd[split:], "crop", bwd_perm), src, split, wrows - split)
    query = acc.astype(jnp.bfloat16)
    nslots = ncrop * CAP
    keys_all = keys_all.reshape(nslots * CT, heads_here, HD)
    vals_all = vals_all.reshape(nslots * CT, heads_here, HD)
    query_row = query.reshape(rows_here, GR, heads_here, HD)
    in_use = (jnp.arange(NB, dtype=jnp.int32)[None, :] < region_len[:, None])[:, :, None]
    hits = region_slots[:, :, None] == jnp.arange(nslots, dtype=jnp.int32)[None, None, :]
    member = jnp.any(hits & in_use, axis=1)
    member = jnp.repeat(member, CT, axis=1)
    scale = 1.0 / HD**0.5
    scores = (
        jnp.einsum("rghe,khe->rhgk", query_row, keys_all, preferred_element_type=jnp.float32)
        * scale
    )
    scores = jnp.where(member[:, None, None, :], scores, jnp.float32(-1e30))
    top = jnp.max(scores, axis=-1, keepdims=True)
    expo = jnp.exp(scores - top)
    weights = (expo / jnp.sum(expo, axis=-1, keepdims=True)).astype(jnp.bfloat16)
    result = jnp.einsum("rhgk,khe->rghe", weights, vals_all, preferred_element_type=jnp.float32)
    return result.astype(jnp.bfloat16).reshape(rows_here * GR, width)


def solution(mesh):
    placed = (
        P("crop", "head"),
        P("crop", "head"),
        P("crop", "head"),
        P("crop", "head"),
        P("crop", "head"),
        P("crop", None, None),
        P("crop", None),
        P("crop"),
    )
    return jax.shard_map(
        body, mesh=mesh, in_specs=placed, out_specs=P("crop", "head"), check_vma=False
    )
```

```python
import jax
import jax.numpy as jnp
from jax import lax
from jax.sharding import PartitionSpec as P

HD = 128
CT = 16
CAP = 2
NB = 8
GR = 32


def ring_order(n):
    half = n // 2
    return [2 * i for i in range(half)] + [2 * i + 1 for i in reversed(range(half))]


def body(
    global_rows,
    crop_tokens,
    query_weight,
    key_weight,
    value_weight,
    fetch_slots,
    region_slots,
    region_len,
):
    width = key_weight.shape[1]
    wrows = key_weight.shape[0]
    heads_here = width // HD
    ncrop = lax.axis_size("crop")
    rows_here = region_slots.shape[0]

    ring = ring_order(ncrop)
    pos_of = [0] * ncrop
    for i, c in enumerate(ring):
        pos_of[c] = i
    me = lax.axis_index("crop")
    pos = jnp.array(pos_of, jnp.int32)[me]
    ring_arr = jnp.array(ring, jnp.int32)
    fwd_perm = [(ring[i], ring[(i + 1) % ncrop]) for i in range(ncrop)]
    bwd_perm = [(ring[i], ring[(i - 1) % ncrop]) for i in range(ncrop)]

    nhead = lax.axis_size("head")
    hme = lax.axis_index("head")

    def head_gather(x):
        full = jnp.zeros((x.shape[0], nhead * x.shape[1]), x.dtype)
        full = lax.dynamic_update_slice(full, x, (0, hme * x.shape[1]))
        for k in range(1, nhead):
            part = lax.ppermute(x, "head", [(j, (j + k) % nhead) for j in range(nhead)])
            full = lax.dynamic_update_slice(full, part, (0, ((hme - k) % nhead) * x.shape[1]))
        return full

    queries_in = head_gather(global_rows)
    picks = fetch_slots[0]
    blocks = crop_tokens.reshape(-1, CT, crop_tokens.shape[1])
    chosen = blocks[picks]
    delivered = lax.all_to_all(chosen, "crop", split_axis=0, concat_axis=0, tiled=True)
    delivered = delivered.reshape(-1, crop_tokens.shape[1])

    steps_fwd = ncrop // 2
    steps_bwd = (ncrop - 1) // 2
    split = wrows // 2

    def ring_pieces(piece):
        got = [(piece, me, 0, wrows)]
        fwd = piece
        bwd = piece
        for k in range(1, steps_bwd + 1):
            fwd = lax.ppermute(fwd, "crop", fwd_perm)
            bwd = lax.ppermute(bwd, "crop", bwd_perm)
            got.append((fwd, ring_arr[(pos - k) % ncrop], 0, wrows))
            got.append((bwd, ring_arr[(pos + k) % ncrop], 0, wrows))
        if steps_fwd > steps_bwd:
            src = ring_arr[(pos - steps_fwd) % ncrop]
            got.append((lax.ppermute(fwd[:split], "crop", fwd_perm), src, 0, split))
            got.append((lax.ppermute(bwd[split:], "crop", bwd_perm), src, split, wrows - split))
        return got

    kv_got = ring_pieces(jnp.concatenate([key_weight, value_weight], axis=1))
    q_piece, last_a, last_b = lax.optimization_barrier(
        (query_weight, kv_got[-1][0], kv_got[-2][0])
    )
    kv_got[-1] = (last_a,) + kv_got[-1][1:]
    kv_got[-2] = (last_b,) + kv_got[-2][1:]
    tokens_in = head_gather(delivered)
    kv_weight = jnp.concatenate([p for p, _, _, _ in kv_got], axis=0)
    tokens_perm = jnp.concatenate(
        [lax.dynamic_slice_in_dim(tokens_in, src * wrows + lo, n, 1) for _, src, lo, n in kv_got],
        axis=1,
    )
    kv = jnp.dot(tokens_perm, kv_weight, preferred_element_type=jnp.float32).astype(jnp.bfloat16)
    incoming = kv.reshape(ncrop, CAP, CT, 2 * width)

    def q_part(acc, piece, src, lo, n):
        cols = lax.dynamic_slice_in_dim(queries_in, src * wrows + lo, n, 1)
        return lax.optimization_barrier(acc + jnp.dot(cols, piece, preferred_element_type=jnp.float32))

    acc = q_part(jnp.zeros((queries_in.shape[0], width), jnp.float32), q_piece, me, 0, wrows)
    fwd = q_piece
    bwd = q_piece
    for k in range(1, steps_bwd + 1):
        fwd = lax.ppermute(fwd, "crop", fwd_perm)
        bwd = lax.ppermute(bwd, "crop", bwd_perm)
        acc = q_part(acc, fwd, ring_arr[(pos - k) % ncrop], 0, wrows)
        acc = q_part(acc, bwd, ring_arr[(pos + k) % ncrop], 0, wrows)
    if steps_fwd > steps_bwd:
        src = ring_arr[(pos - steps_fwd) % ncrop]
        acc = q_part(acc, lax.ppermute(fwd[:split], "crop", fwd_perm), src, 0, split)
        acc = q_part(acc, lax.ppermute(bwd[split:], "crop", bwd_perm), src, split, wrows - split)
    query = acc.astype(jnp.bfloat16)
    nslots = ncrop * CAP
    keys_all = incoming[..., :width].reshape(nslots * CT, heads_here, HD)
    vals_all = incoming[..., width:].reshape(nslots * CT, heads_here, HD)
    query_row = query.reshape(rows_here, GR, heads_here, HD)
    in_use = (jnp.arange(NB, dtype=jnp.int32)[None, :] < region_len[:, None])[:, :, None]
    hits = region_slots[:, :, None] == jnp.arange(nslots, dtype=jnp.int32)[None, None, :]
    member = jnp.any(hits & in_use, axis=1)
    member = jnp.repeat(member, CT, axis=1)
    scale = 1.0 / HD**0.5
    scores = (
        jnp.einsum("rghe,khe->rhgk", query_row, keys_all, preferred_element_type=jnp.float32)
        * scale
    )
    scores = jnp.where(member[:, None, None, :], scores, jnp.float32(-1e30))
    top = jnp.max(scores, axis=-1, keepdims=True)
    expo = jnp.exp(scores - top)
    weights = (expo / jnp.sum(expo, axis=-1, keepdims=True)).astype(jnp.bfloat16)
    result = jnp.einsum("rhgk,khe->rghe", weights, vals_all, preferred_element_type=jnp.float32)
    return result.astype(jnp.bfloat16).reshape(rows_here * GR, width)


def solution(mesh):
    placed = (
        P("crop", "head"),
        P("crop", "head"),
        P("crop", "head"),
        P("crop", "head"),
        P("crop", "head"),
        P("crop", None, None),
        P("crop", None),
        P("crop"),
    )
    return jax.shard_map(
        body, mesh=mesh, in_specs=placed, out_specs=P("crop", "head"), check_vma=False
    )
```

```python
import jax
import jax.numpy as jnp
from jax import lax
from jax.sharding import PartitionSpec as P

HD = 128
CT = 16
CAP = 2
NB = 8
GR = 32


def ring_order(n):
    half = n // 2
    return [2 * i for i in range(half)] + [2 * i + 1 for i in reversed(range(half))]


def body(
    global_rows,
    crop_tokens,
    query_weight,
    key_weight,
    value_weight,
    fetch_slots,
    region_slots,
    region_len,
):
    width = key_weight.shape[1]
    wrows = key_weight.shape[0]
    heads_here = width // HD
    ncrop = lax.axis_size("crop")
    rows_here = region_slots.shape[0]

    ring = ring_order(ncrop)
    pos_of = [0] * ncrop
    for i, c in enumerate(ring):
        pos_of[c] = i
    me = lax.axis_index("crop")
    pos = jnp.array(pos_of, jnp.int32)[me]
    ring_arr = jnp.array(ring, jnp.int32)
    fwd_perm = [(ring[i], ring[(i + 1) % ncrop]) for i in range(ncrop)]
    bwd_perm = [(ring[i], ring[(i - 1) % ncrop]) for i in range(ncrop)]

    nhead = lax.axis_size("head")
    hme = lax.axis_index("head")

    def head_gather(x):
        full = jnp.zeros((x.shape[0], nhead * x.shape[1]), x.dtype)
        full = lax.dynamic_update_slice(full, x, (0, hme * x.shape[1]))
        for k in range(1, nhead):
            part = lax.ppermute(x, "head", [(j, (j + k) % nhead) for j in range(nhead)])
            full = lax.dynamic_update_slice(full, part, (0, ((hme - k) % nhead) * x.shape[1]))
        return full

    queries_in = head_gather(global_rows)
    picks = fetch_slots[0]
    blocks = crop_tokens.reshape(-1, CT, crop_tokens.shape[1])
    chosen = blocks[picks]
    delivered = lax.all_to_all(chosen, "crop", split_axis=0, concat_axis=0, tiled=True)
    delivered = delivered.reshape(-1, crop_tokens.shape[1])

    steps_fwd = ncrop // 2
    steps_bwd = (ncrop - 1) // 2
    split = wrows // 2

    def ring_pieces(piece):
        got = [(piece, me, 0, wrows)]
        fwd = piece
        bwd = piece
        for k in range(1, steps_bwd + 1):
            fwd = lax.ppermute(fwd, "crop", fwd_perm)
            bwd = lax.ppermute(bwd, "crop", bwd_perm)
            got.append((fwd, ring_arr[(pos - k) % ncrop], 0, wrows))
            got.append((bwd, ring_arr[(pos + k) % ncrop], 0, wrows))
        if steps_fwd > steps_bwd:
            src = ring_arr[(pos - steps_fwd) % ncrop]
            got.append((lax.ppermute(fwd[:split], "crop", fwd_perm), src, 0, split))
            got.append((lax.ppermute(bwd[split:], "crop", bwd_perm), src, split, wrows - split))
        return got

    kv_got = ring_pieces(jnp.concatenate([key_weight, value_weight], axis=1))
    q_piece, last_a, last_b = lax.optimization_barrier(
        (query_weight, kv_got[-1][0], kv_got[-2][0])
    )
    kv_got[-1] = (last_a,) + kv_got[-1][1:]
    kv_got[-2] = (last_b,) + kv_got[-2][1:]
    tokens_in = head_gather(delivered)
    kv_weight = jnp.concatenate([p for p, _, _, _ in kv_got], axis=0)
    tokens_perm = jnp.concatenate(
        [lax.dynamic_slice_in_dim(tokens_in, src * wrows + lo, n, 1) for _, src, lo, n in kv_got],
        axis=1,
    )
    kv = jnp.dot(tokens_perm, kv_weight, preferred_element_type=jnp.float32).astype(jnp.bfloat16)
    incoming = kv.reshape(ncrop, CAP, CT, 2 * width)

    def q_part(acc, piece, src, lo, n):
        cols = lax.dynamic_slice_in_dim(queries_in, src * wrows + lo, n, 1)
        piece = piece.reshape(n, heads_here, HD)
        part = jnp.einsum("rf,fhe->hre", cols, piece, preferred_element_type=jnp.float32)
        return lax.optimization_barrier(acc + part)

    acc = jnp.zeros((heads_here, queries_in.shape[0], HD), jnp.float32)
    acc = q_part(acc, q_piece, me, 0, wrows)
    fwd = q_piece
    bwd = q_piece
    for k in range(1, steps_bwd + 1):
        fwd = lax.ppermute(fwd, "crop", fwd_perm)
        bwd = lax.ppermute(bwd, "crop", bwd_perm)
        acc = q_part(acc, fwd, ring_arr[(pos - k) % ncrop], 0, wrows)
        acc = q_part(acc, bwd, ring_arr[(pos + k) % ncrop], 0, wrows)
    if steps_fwd > steps_bwd:
        src = ring_arr[(pos - steps_fwd) % ncrop]
        acc = q_part(acc, lax.ppermute(fwd[:split], "crop", fwd_perm), src, 0, split)
        acc = q_part(acc, lax.ppermute(bwd[split:], "crop", bwd_perm), src, split, wrows - split)
    query = acc.astype(jnp.bfloat16)
    nslots = ncrop * CAP
    keys_all = incoming[..., :width].reshape(nslots * CT, heads_here, HD)
    vals_all = incoming[..., width:].reshape(nslots * CT, heads_here, HD)
    query_row = query.reshape(heads_here, rows_here, GR, HD)
    in_use = (jnp.arange(NB, dtype=jnp.int32)[None, :] < region_len[:, None])[:, :, None]
    hits = region_slots[:, :, None] == jnp.arange(nslots, dtype=jnp.int32)[None, None, :]
    member = jnp.any(hits & in_use, axis=1)
    member = jnp.repeat(member, CT, axis=1)
    scale = 1.0 / HD**0.5
    scores = (
        jnp.einsum("hrge,khe->rhgk", query_row, keys_all, preferred_element_type=jnp.float32)
        * scale
    )
    scores = jnp.where(member[:, None, None, :], scores, jnp.float32(-1e30))
    top = jnp.max(scores, axis=-1, keepdims=True)
    expo = jnp.exp(scores - top)
    weights = (expo / jnp.sum(expo, axis=-1, keepdims=True)).astype(jnp.bfloat16)
    result = jnp.einsum("rhgk,khe->rghe", weights, vals_all, preferred_element_type=jnp.float32)
    return result.astype(jnp.bfloat16).reshape(rows_here * GR, width)


def solution(mesh):
    placed = (
        P("crop", "head"),
        P("crop", "head"),
        P("crop", "head"),
        P("crop", "head"),
        P("crop", "head"),
        P("crop", None, None),
        P("crop", None),
        P("crop"),
    )
    return jax.shard_map(
        body, mesh=mesh, in_specs=placed, out_specs=P("crop", "head"), check_vma=False
    )
```

```python
import jax
import jax.numpy as jnp
from jax import lax
from jax.sharding import PartitionSpec as P

HD = 128
CT = 16
CAP = 2
NB = 8
GR = 32


def ring_order(n):
    half = n // 2
    return [2 * i for i in range(half)] + [2 * i + 1 for i in reversed(range(half))]


def body(
    global_rows,
    crop_tokens,
    query_weight,
    key_weight,
    value_weight,
    fetch_slots,
    region_slots,
    region_len,
):
    width = key_weight.shape[1]
    wrows = key_weight.shape[0]
    heads_here = width // HD
    ncrop = lax.axis_size("crop")
    rows_here = region_slots.shape[0]

    ring = ring_order(ncrop)
    pos_of = [0] * ncrop
    for i, c in enumerate(ring):
        pos_of[c] = i
    me = lax.axis_index("crop")
    pos = jnp.array(pos_of, jnp.int32)[me]
    ring_arr = jnp.array(ring, jnp.int32)
    fwd_perm = [(ring[i], ring[(i + 1) % ncrop]) for i in range(ncrop)]
    bwd_perm = [(ring[i], ring[(i - 1) % ncrop]) for i in range(ncrop)]

    nhead = lax.axis_size("head")
    hme = lax.axis_index("head")

    def head_gather(x):
        full = jnp.zeros((x.shape[0], nhead * x.shape[1]), x.dtype)
        full = lax.dynamic_update_slice(full, x, (0, hme * x.shape[1]))
        for k in range(1, nhead):
            part = lax.ppermute(x, "head", [(j, (j + k) % nhead) for j in range(nhead)])
            full = lax.dynamic_update_slice(full, part, (0, ((hme - k) % nhead) * x.shape[1]))
        return full

    queries_in = head_gather(global_rows)
    picks = fetch_slots[0]
    blocks = crop_tokens.reshape(-1, CT, crop_tokens.shape[1])
    chosen = blocks[picks]
    delivered = lax.all_to_all(chosen, "crop", split_axis=0, concat_axis=0, tiled=True)
    delivered = delivered.reshape(-1, crop_tokens.shape[1])

    steps_fwd = ncrop // 2
    steps_bwd = (ncrop - 1) // 2
    split = wrows // 2

    def ring_pieces(piece):
        got = [(piece, me, 0, wrows)]
        fwd = piece
        bwd = piece
        for k in range(1, steps_bwd + 1):
            fwd = lax.ppermute(fwd, "crop", fwd_perm)
            bwd = lax.ppermute(bwd, "crop", bwd_perm)
            got.append((fwd, ring_arr[(pos - k) % ncrop], 0, wrows))
            got.append((bwd, ring_arr[(pos + k) % ncrop], 0, wrows))
        if steps_fwd > steps_bwd:
            src = ring_arr[(pos - steps_fwd) % ncrop]
            got.append((lax.ppermute(fwd[:split], "crop", fwd_perm), src, 0, split))
            got.append((lax.ppermute(bwd[split:], "crop", bwd_perm), src, split, wrows - split))
        return got

    kv_got = ring_pieces(lax.optimization_barrier(jnp.concatenate([key_weight, value_weight], axis=1)))
    q_piece, last_a, last_b = lax.optimization_barrier(
        (query_weight, kv_got[-1][0], kv_got[-2][0])
    )
    kv_got[-1] = (last_a,) + kv_got[-1][1:]
    kv_got[-2] = (last_b,) + kv_got[-2][1:]
    tokens_in = head_gather(delivered)
    kv_weight = jnp.concatenate([p for p, _, _, _ in kv_got], axis=0)
    tokens_perm = jnp.concatenate(
        [lax.dynamic_slice_in_dim(tokens_in, src * wrows + lo, n, 1) for _, src, lo, n in kv_got],
        axis=1,
    )
    kv = jnp.dot(tokens_perm, kv_weight, preferred_element_type=jnp.float32).astype(jnp.bfloat16)
    incoming = kv.reshape(ncrop, CAP, CT, 2 * width)

    def q_part(acc, piece, src, lo, n):
        cols = lax.dynamic_slice_in_dim(queries_in, src * wrows + lo, n, 1)
        return lax.optimization_barrier(acc + jnp.dot(cols, piece, preferred_element_type=jnp.float32))

    acc = q_part(jnp.zeros((queries_in.shape[0], width), jnp.float32), q_piece, me, 0, wrows)
    fwd = q_piece
    bwd = q_piece
    for k in range(1, steps_bwd + 1):
        fwd = lax.ppermute(fwd, "crop", fwd_perm)
        bwd = lax.ppermute(bwd, "crop", bwd_perm)
        acc = q_part(acc, fwd, ring_arr[(pos - k) % ncrop], 0, wrows)
        acc = q_part(acc, bwd, ring_arr[(pos + k) % ncrop], 0, wrows)
    if steps_fwd > steps_bwd:
        src = ring_arr[(pos - steps_fwd) % ncrop]
        acc = q_part(acc, lax.ppermute(fwd[:split], "crop", fwd_perm), src, 0, split)
        acc = q_part(acc, lax.ppermute(bwd[split:], "crop", bwd_perm), src, split, wrows - split)
    query = acc.astype(jnp.bfloat16)
    nslots = ncrop * CAP
    keys_all = incoming[..., :width].reshape(nslots * CT, heads_here, HD)
    vals_all = incoming[..., width:].reshape(nslots * CT, heads_here, HD)
    query_row = query.reshape(rows_here, GR, heads_here, HD)
    in_use = (jnp.arange(NB, dtype=jnp.int32)[None, :] < region_len[:, None])[:, :, None]
    hits = region_slots[:, :, None] == jnp.arange(nslots, dtype=jnp.int32)[None, None, :]
    member = jnp.any(hits & in_use, axis=1)
    member = jnp.repeat(member, CT, axis=1)
    scale = 1.0 / HD**0.5
    scores = (
        jnp.einsum("rghe,khe->rhgk", query_row, keys_all, preferred_element_type=jnp.float32)
        * scale
    )
    scores = jnp.where(member[:, None, None, :], scores, jnp.float32(-1e30))
    top = jnp.max(scores, axis=-1, keepdims=True)
    expo = jnp.exp(scores - top)
    weights = (expo / jnp.sum(expo, axis=-1, keepdims=True)).astype(jnp.bfloat16)
    result = jnp.einsum("rhgk,khe->rghe", weights, vals_all, preferred_element_type=jnp.float32)
    return result.astype(jnp.bfloat16).reshape(rows_here * GR, width)


def solution(mesh):
    placed = (
        P("crop", "head"),
        P("crop", "head"),
        P("crop", "head"),
        P("crop", "head"),
        P("crop", "head"),
        P("crop", None, None),
        P("crop", None),
        P("crop"),
    )
    return jax.shard_map(
        body, mesh=mesh, in_specs=placed, out_specs=P("crop", "head"), check_vma=False
    )
```

```python
import jax
import jax.numpy as jnp
from jax import lax
from jax.sharding import PartitionSpec as P

HD = 128
CT = 16
CAP = 2
NB = 8
GR = 32


def ring_order(n):
    half = n // 2
    return [2 * i for i in range(half)] + [2 * i + 1 for i in reversed(range(half))]


def body(
    global_rows,
    crop_tokens,
    query_weight,
    key_weight,
    value_weight,
    fetch_slots,
    region_slots,
    region_len,
):
    width = key_weight.shape[1]
    wrows = key_weight.shape[0]
    heads_here = width // HD
    ncrop = lax.axis_size("crop")
    rows_here = region_slots.shape[0]

    ring = ring_order(ncrop)
    pos_of = [0] * ncrop
    for i, c in enumerate(ring):
        pos_of[c] = i
    me = lax.axis_index("crop")
    pos = jnp.array(pos_of, jnp.int32)[me]
    ring_arr = jnp.array(ring, jnp.int32)
    fwd_perm = [(ring[i], ring[(i + 1) % ncrop]) for i in range(ncrop)]
    bwd_perm = [(ring[i], ring[(i - 1) % ncrop]) for i in range(ncrop)]

    nhead = lax.axis_size("head")
    hme = lax.axis_index("head")

    def head_gather(x):
        full = jnp.zeros((x.shape[0], nhead * x.shape[1]), x.dtype)
        full = lax.dynamic_update_slice(full, x, (0, hme * x.shape[1]))
        for k in range(1, nhead):
            part = lax.ppermute(x, "head", [(j, (j + k) % nhead) for j in range(nhead)])
            full = lax.dynamic_update_slice(full, part, (0, ((hme - k) % nhead) * x.shape[1]))
        return full

    queries_in = head_gather(global_rows)
    picks = fetch_slots[0]
    blocks = crop_tokens.reshape(-1, CT, crop_tokens.shape[1])
    chosen = blocks[picks]
    delivered = lax.all_to_all(chosen, "crop", split_axis=0, concat_axis=0, tiled=True)
    delivered = delivered.reshape(-1, crop_tokens.shape[1])

    steps_fwd = ncrop // 2
    steps_bwd = (ncrop - 1) // 2
    split = wrows // 2

    def ring_pieces(piece):
        got = [(piece, me, 0, wrows)]
        fwd = piece
        bwd = piece
        for k in range(1, steps_bwd + 1):
            fwd = lax.ppermute(fwd, "crop", fwd_perm)
            bwd = lax.ppermute(bwd, "crop", bwd_perm)
            got.append((fwd, ring_arr[(pos - k) % ncrop], 0, wrows))
            got.append((bwd, ring_arr[(pos + k) % ncrop], 0, wrows))
        if steps_fwd > steps_bwd:
            src = ring_arr[(pos - steps_fwd) % ncrop]
            got.append((lax.ppermute(fwd[:split], "crop", fwd_perm), src, 0, split))
            got.append((lax.ppermute(bwd[split:], "crop", bwd_perm), src, split, wrows - split))
        return got

    k_got = ring_pieces(key_weight)
    v_piece, k_last, k_prev = lax.optimization_barrier((value_weight, k_got[-1][0], k_got[-2][0]))
    k_got[-1] = (k_last,) + k_got[-1][1:]
    k_got[-2] = (k_prev,) + k_got[-2][1:]
    v_got = ring_pieces(v_piece)
    q_piece, v_last, v_prev = lax.optimization_barrier((query_weight, v_got[-1][0], v_got[-2][0]))
    v_got[-1] = (v_last,) + v_got[-1][1:]
    v_got[-2] = (v_prev,) + v_got[-2][1:]
    tokens_in = head_gather(delivered)
    tokens_perm = jnp.concatenate(
        [lax.dynamic_slice_in_dim(tokens_in, src * wrows + lo, n, 1) for _, src, lo, n in k_got],
        axis=1,
    )

    def project(got):
        weight = jnp.concatenate([p for p, _, _, _ in got], axis=0)
        out = jnp.dot(tokens_perm, weight, preferred_element_type=jnp.float32)
        return out.astype(jnp.bfloat16)

    keys_all = project(k_got)
    vals_all = project(v_got)

    def q_part(acc, piece, src, lo, n):
        cols = lax.dynamic_slice_in_dim(queries_in, src * wrows + lo, n, 1)
        return lax.optimization_barrier(acc + jnp.dot(cols, piece, preferred_element_type=jnp.float32))

    acc = q_part(jnp.zeros((queries_in.shape[0], width), jnp.float32), q_piece, me, 0, wrows)
    fwd = q_piece
    bwd = q_piece
    for k in range(1, steps_bwd + 1):
        fwd = lax.ppermute(fwd, "crop", fwd_perm)
        bwd = lax.ppermute(bwd, "crop", bwd_perm)
        acc = q_part(acc, fwd, ring_arr[(pos - k) % ncrop], 0, wrows)
        acc = q_part(acc, bwd, ring_arr[(pos + k) % ncrop], 0, wrows)
    if steps_fwd > steps_bwd:
        src = ring_arr[(pos - steps_fwd) % ncrop]
        acc = q_part(acc, lax.ppermute(fwd[:split], "crop", fwd_perm), src, 0, split)
        acc = q_part(acc, lax.ppermute(bwd[split:], "crop", bwd_perm), src, split, wrows - split)
    query = acc.astype(jnp.bfloat16)
    nslots = ncrop * CAP
    keys_all = keys_all.reshape(nslots * CT, heads_here, HD)
    vals_all = vals_all.reshape(nslots * CT, heads_here, HD)
    query_row = query.reshape(rows_here, GR, heads_here, HD)
    in_use = (jnp.arange(NB, dtype=jnp.int32)[None, :] < region_len[:, None])[:, :, None]
    hits = region_slots[:, :, None] == jnp.arange(nslots, dtype=jnp.int32)[None, None, :]
    member = jnp.any(hits & in_use, axis=1)
    member = jnp.repeat(member, CT, axis=1)
    scale = 1.0 / HD**0.5
    scores = (
        jnp.einsum("rghe,khe->rhgk", query_row, keys_all, preferred_element_type=jnp.float32)
        * scale
    )
    scores = jnp.where(member[:, None, None, :], scores, jnp.float32(-1e30))
    top = jnp.max(scores, axis=-1, keepdims=True)
    expo = jnp.exp(scores - top)
    weights = (expo / jnp.sum(expo, axis=-1, keepdims=True)).astype(jnp.bfloat16)
    result = jnp.einsum("rhgk,khe->rghe", weights, vals_all, preferred_element_type=jnp.float32)
    return result.astype(jnp.bfloat16).reshape(rows_here * GR, width)


def solution(mesh):
    placed = (
        P("crop", "head"),
        P("crop", "head"),
        P("crop", "head"),
        P("crop", "head"),
        P("crop", "head"),
        P("crop", None, None),
        P("crop", None),
        P("crop"),
    )
    return jax.shard_map(
        body, mesh=mesh, in_specs=placed, out_specs=P("crop", "head"), check_vma=False
    )
```

```python
import jax
import jax.numpy as jnp
from jax import lax
from jax.sharding import PartitionSpec as P

HD = 128
CT = 16
CAP = 2
NB = 8
GR = 32


def ring_order(n):
    half = n // 2
    return [2 * i for i in range(half)] + [2 * i + 1 for i in reversed(range(half))]


def body(
    global_rows,
    crop_tokens,
    query_weight,
    key_weight,
    value_weight,
    fetch_slots,
    region_slots,
    region_len,
):
    width = key_weight.shape[1]
    wrows = key_weight.shape[0]
    heads_here = width // HD
    ncrop = lax.axis_size("crop")
    rows_here = region_slots.shape[0]

    ring = ring_order(ncrop)
    pos_of = [0] * ncrop
    for i, c in enumerate(ring):
        pos_of[c] = i
    me = lax.axis_index("crop")
    pos = jnp.array(pos_of, jnp.int32)[me]
    ring_arr = jnp.array(ring, jnp.int32)
    fwd_perm = [(ring[i], ring[(i + 1) % ncrop]) for i in range(ncrop)]
    bwd_perm = [(ring[i], ring[(i - 1) % ncrop]) for i in range(ncrop)]

    nhead = lax.axis_size("head")
    hme = lax.axis_index("head")

    def head_gather(x):
        full = jnp.zeros((x.shape[0], nhead * x.shape[1]), x.dtype)
        full = lax.dynamic_update_slice(full, x, (0, hme * x.shape[1]))
        for k in range(1, nhead):
            part = lax.ppermute(x, "head", [(j, (j + k) % nhead) for j in range(nhead)])
            full = lax.dynamic_update_slice(full, part, (0, ((hme - k) % nhead) * x.shape[1]))
        return full

    queries_in = head_gather(global_rows)
    picks = fetch_slots[0]
    blocks = crop_tokens.reshape(-1, CT, crop_tokens.shape[1])
    chosen = blocks[picks]
    delivered = lax.all_to_all(chosen, "crop", split_axis=0, concat_axis=0, tiled=True)
    delivered = delivered.reshape(-1, crop_tokens.shape[1])

    steps_fwd = ncrop // 2
    steps_bwd = (ncrop - 1) // 2
    split = wrows // 2

    def ring_pieces(piece):
        two = piece.reshape(2, split, piece.shape[1])
        got = [(piece, me, 0, wrows)]
        fwd = two
        bwd = two
        for k in range(1, steps_bwd + 1):
            fwd = lax.ppermute(fwd, "crop", fwd_perm)
            bwd = lax.ppermute(bwd, "crop", bwd_perm)
            got.append((fwd.reshape(wrows, -1), ring_arr[(pos - k) % ncrop], 0, wrows))
            got.append((bwd.reshape(wrows, -1), ring_arr[(pos + k) % ncrop], 0, wrows))
        if steps_fwd > steps_bwd:
            src = ring_arr[(pos - steps_fwd) % ncrop]
            got.append((lax.ppermute(fwd[0], "crop", fwd_perm), src, 0, split))
            got.append((lax.ppermute(bwd[1], "crop", bwd_perm), src, split, wrows - split))
        return got

    kv_got = ring_pieces(lax.optimization_barrier(jnp.concatenate([key_weight, value_weight], axis=1)))
    q_piece, last_a, last_b = lax.optimization_barrier(
        (query_weight, kv_got[-1][0], kv_got[-2][0])
    )
    kv_got[-1] = (last_a,) + kv_got[-1][1:]
    kv_got[-2] = (last_b,) + kv_got[-2][1:]
    tokens_in = head_gather(delivered)
    kv_weight = jnp.concatenate([p for p, _, _, _ in kv_got], axis=0)
    tokens_perm = jnp.concatenate(
        [lax.dynamic_slice_in_dim(tokens_in, src * wrows + lo, n, 1) for _, src, lo, n in kv_got],
        axis=1,
    )
    kv = jnp.dot(tokens_perm, kv_weight, preferred_element_type=jnp.float32).astype(jnp.bfloat16)
    incoming = kv.reshape(ncrop, CAP, CT, 2 * width)

    def q_part(acc, piece, src, lo, n):
        cols = lax.dynamic_slice_in_dim(queries_in, src * wrows + lo, n, 1)
        return lax.optimization_barrier(acc + jnp.dot(cols, piece, preferred_element_type=jnp.float32))

    acc = q_part(jnp.zeros((queries_in.shape[0], width), jnp.float32), q_piece, me, 0, wrows)
    fwd = q_piece.reshape(2, split, width)
    bwd = fwd
    for k in range(1, steps_bwd + 1):
        fwd = lax.ppermute(fwd, "crop", fwd_perm)
        bwd = lax.ppermute(bwd, "crop", bwd_perm)
        acc = q_part(acc, fwd.reshape(wrows, width), ring_arr[(pos - k) % ncrop], 0, wrows)
        acc = q_part(acc, bwd.reshape(wrows, width), ring_arr[(pos + k) % ncrop], 0, wrows)
    if steps_fwd > steps_bwd:
        src = ring_arr[(pos - steps_fwd) % ncrop]
        acc = q_part(acc, lax.ppermute(fwd[0], "crop", fwd_perm), src, 0, split)
        acc = q_part(acc, lax.ppermute(bwd[1], "crop", bwd_perm), src, split, wrows - split)
    query = acc.astype(jnp.bfloat16)
    nslots = ncrop * CAP
    keys_all = incoming[..., :width].reshape(nslots * CT, heads_here, HD)
    vals_all = incoming[..., width:].reshape(nslots * CT, heads_here, HD)
    query_row = query.reshape(rows_here, GR, heads_here, HD)
    in_use = (jnp.arange(NB, dtype=jnp.int32)[None, :] < region_len[:, None])[:, :, None]
    hits = region_slots[:, :, None] == jnp.arange(nslots, dtype=jnp.int32)[None, None, :]
    member = jnp.any(hits & in_use, axis=1)
    member = jnp.repeat(member, CT, axis=1)
    scale = 1.0 / HD**0.5
    scores = (
        jnp.einsum("rghe,khe->rhgk", query_row, keys_all, preferred_element_type=jnp.float32)
        * scale
    )
    scores = jnp.where(member[:, None, None, :], scores, jnp.float32(-1e30))
    top = jnp.max(scores, axis=-1, keepdims=True)
    expo = jnp.exp(scores - top)
    weights = (expo / jnp.sum(expo, axis=-1, keepdims=True)).astype(jnp.bfloat16)
    result = jnp.einsum("rhgk,khe->rghe", weights, vals_all, preferred_element_type=jnp.float32)
    return result.astype(jnp.bfloat16).reshape(rows_here * GR, width)


def solution(mesh):
    placed = (
        P("crop", "head"),
        P("crop", "head"),
        P("crop", "head"),
        P("crop", "head"),
        P("crop", "head"),
        P("crop", None, None),
        P("crop", None),
        P("crop"),
    )
    return jax.shard_map(
        body, mesh=mesh, in_specs=placed, out_specs=P("crop", "head"), check_vma=False
    )
```

```python
import jax
import jax.numpy as jnp
from jax import lax
from jax.sharding import PartitionSpec as P

HD = 128
CT = 16
CAP = 2
NB = 8
GR = 32


def ring_order(n):
    half = n // 2
    return [2 * i for i in range(half)] + [2 * i + 1 for i in reversed(range(half))]


def body(
    global_rows,
    crop_tokens,
    query_weight,
    key_weight,
    value_weight,
    fetch_slots,
    region_slots,
    region_len,
):
    width = key_weight.shape[1]
    wrows = key_weight.shape[0]
    heads_here = width // HD
    ncrop = lax.axis_size("crop")
    rows_here = region_slots.shape[0]

    ring = ring_order(ncrop)
    pos_of = [0] * ncrop
    for i, c in enumerate(ring):
        pos_of[c] = i
    me = lax.axis_index("crop")
    pos = jnp.array(pos_of, jnp.int32)[me]
    ring_arr = jnp.array(ring, jnp.int32)
    fwd_perm = [(ring[i], ring[(i + 1) % ncrop]) for i in range(ncrop)]
    bwd_perm = [(ring[i], ring[(i - 1) % ncrop]) for i in range(ncrop)]

    nhead = lax.axis_size("head")
    hme = lax.axis_index("head")

    def head_gather(x):
        full = jnp.zeros((x.shape[0], nhead * x.shape[1]), x.dtype)
        full = lax.dynamic_update_slice(full, x, (0, hme * x.shape[1]))
        for k in range(1, nhead):
            part = lax.ppermute(x, "head", [(j, (j + k) % nhead) for j in range(nhead)])
            full = lax.dynamic_update_slice(full, part, (0, ((hme - k) % nhead) * x.shape[1]))
        return full

    queries_in = head_gather(global_rows)
    picks = fetch_slots[0]
    blocks = crop_tokens.reshape(-1, CT, crop_tokens.shape[1])
    chosen = blocks[picks]
    delivered = lax.all_to_all(chosen, "crop", split_axis=0, concat_axis=0, tiled=True)
    delivered = delivered.reshape(-1, crop_tokens.shape[1])

    steps_fwd = ncrop // 2
    steps_bwd = (ncrop - 1) // 2
    split = wrows // 2

    def ring_pieces(piece):
        got = [(piece, me, 0, wrows)]
        fwd = piece
        bwd = piece
        for k in range(1, steps_bwd + 1):
            fwd = lax.ppermute(fwd, "crop", fwd_perm)
            bwd = lax.ppermute(bwd, "crop", bwd_perm)
            got.append((fwd, ring_arr[(pos - k) % ncrop], 0, wrows))
            got.append((bwd, ring_arr[(pos + k) % ncrop], 0, wrows))
        if steps_fwd > steps_bwd:
            src = ring_arr[(pos - steps_fwd) % ncrop]
            got.append((lax.ppermute(fwd[:split], "crop", fwd_perm), src, 0, split))
            got.append((lax.ppermute(bwd[split:], "crop", bwd_perm), src, split, wrows - split))
        return got

    kv_got = ring_pieces(lax.optimization_barrier(jnp.concatenate([key_weight, value_weight], axis=1)))
    at = -3 if steps_fwd > steps_bwd else -1
    q_piece, last_a, last_b = lax.optimization_barrier(
        (query_weight, kv_got[at][0], kv_got[at - 1][0])
    )
    kv_got[at] = (last_a,) + kv_got[at][1:]
    kv_got[at - 1] = (last_b,) + kv_got[at - 1][1:]
    tokens_in = head_gather(delivered)
    kv_weight = jnp.concatenate([p for p, _, _, _ in kv_got], axis=0)
    tokens_perm = jnp.concatenate(
        [lax.dynamic_slice_in_dim(tokens_in, src * wrows + lo, n, 1) for _, src, lo, n in kv_got],
        axis=1,
    )
    kv = jnp.dot(tokens_perm, kv_weight, preferred_element_type=jnp.float32).astype(jnp.bfloat16)
    incoming = kv.reshape(ncrop, CAP, CT, 2 * width)

    def q_part(acc, piece, src, lo, n):
        cols = lax.dynamic_slice_in_dim(queries_in, src * wrows + lo, n, 1)
        return lax.optimization_barrier(acc + jnp.dot(cols, piece, preferred_element_type=jnp.float32))

    acc = q_part(jnp.zeros((queries_in.shape[0], width), jnp.float32), q_piece, me, 0, wrows)
    fwd = q_piece
    bwd = q_piece
    for k in range(1, steps_bwd + 1):
        fwd = lax.ppermute(fwd, "crop", fwd_perm)
        bwd = lax.ppermute(bwd, "crop", bwd_perm)
        acc = q_part(acc, fwd, ring_arr[(pos - k) % ncrop], 0, wrows)
        acc = q_part(acc, bwd, ring_arr[(pos + k) % ncrop], 0, wrows)
    if steps_fwd > steps_bwd:
        src = ring_arr[(pos - steps_fwd) % ncrop]
        acc = q_part(acc, lax.ppermute(fwd[:split], "crop", fwd_perm), src, 0, split)
        acc = q_part(acc, lax.ppermute(bwd[split:], "crop", bwd_perm), src, split, wrows - split)
    query = acc.astype(jnp.bfloat16)
    nslots = ncrop * CAP
    keys_all = incoming[..., :width].reshape(nslots * CT, heads_here, HD)
    vals_all = incoming[..., width:].reshape(nslots * CT, heads_here, HD)
    query_row = query.reshape(rows_here, GR, heads_here, HD)
    in_use = (jnp.arange(NB, dtype=jnp.int32)[None, :] < region_len[:, None])[:, :, None]
    hits = region_slots[:, :, None] == jnp.arange(nslots, dtype=jnp.int32)[None, None, :]
    member = jnp.any(hits & in_use, axis=1)
    member = jnp.repeat(member, CT, axis=1)
    scale = 1.0 / HD**0.5
    scores = (
        jnp.einsum("rghe,khe->rhgk", query_row, keys_all, preferred_element_type=jnp.float32)
        * scale
    )
    scores = jnp.where(member[:, None, None, :], scores, jnp.float32(-1e30))
    top = jnp.max(scores, axis=-1, keepdims=True)
    expo = jnp.exp(scores - top)
    weights = (expo / jnp.sum(expo, axis=-1, keepdims=True)).astype(jnp.bfloat16)
    result = jnp.einsum("rhgk,khe->rghe", weights, vals_all, preferred_element_type=jnp.float32)
    return result.astype(jnp.bfloat16).reshape(rows_here * GR, width)


def solution(mesh):
    placed = (
        P("crop", "head"),
        P("crop", "head"),
        P("crop", "head"),
        P("crop", "head"),
        P("crop", "head"),
        P("crop", None, None),
        P("crop", None),
        P("crop"),
    )
    return jax.shard_map(
        body, mesh=mesh, in_specs=placed, out_specs=P("crop", "head"), check_vma=False
    )
```

```python
import jax
import jax.numpy as jnp
from jax import lax
from jax.sharding import PartitionSpec as P

HD = 128
CT = 16
CAP = 2
NB = 8
GR = 32


def ring_order(n):
    half = n // 2
    return [2 * i for i in range(half)] + [2 * i + 1 for i in reversed(range(half))]


def body(
    global_rows,
    crop_tokens,
    query_weight,
    key_weight,
    value_weight,
    fetch_slots,
    region_slots,
    region_len,
):
    width = key_weight.shape[1]
    wrows = key_weight.shape[0]
    heads_here = width // HD
    ncrop = lax.axis_size("crop")
    rows_here = region_slots.shape[0]

    ring = ring_order(ncrop)
    pos_of = [0] * ncrop
    for i, c in enumerate(ring):
        pos_of[c] = i
    me = lax.axis_index("crop")
    pos = jnp.array(pos_of, jnp.int32)[me]
    ring_arr = jnp.array(ring, jnp.int32)
    fwd_perm = [(ring[i], ring[(i + 1) % ncrop]) for i in range(ncrop)]
    bwd_perm = [(ring[i], ring[(i - 1) % ncrop]) for i in range(ncrop)]

    nhead = lax.axis_size("head")
    hme = lax.axis_index("head")

    def head_gather(x):
        full = jnp.zeros((x.shape[0], nhead * x.shape[1]), x.dtype)
        full = lax.dynamic_update_slice(full, x, (0, hme * x.shape[1]))
        for k in range(1, nhead):
            part = lax.ppermute(x, "head", [(j, (j + k) % nhead) for j in range(nhead)])
            full = lax.dynamic_update_slice(full, part, (0, ((hme - k) % nhead) * x.shape[1]))
        return full

    queries_in = head_gather(global_rows)
    picks = fetch_slots[0]
    blocks = crop_tokens.reshape(-1, CT, crop_tokens.shape[1])
    chosen = blocks[picks]
    delivered = lax.all_to_all(chosen, "crop", split_axis=0, concat_axis=0, tiled=True)
    delivered = delivered.reshape(-1, crop_tokens.shape[1])

    steps_fwd = ncrop // 2
    steps_bwd = (ncrop - 1) // 2
    split = wrows // 2

    def ring_pieces(piece):
        got = [(piece, me, 0, wrows)]
        fwd = piece
        bwd = piece
        for k in range(1, steps_bwd + 1):
            fwd = lax.ppermute(fwd, "crop", fwd_perm)
            bwd = lax.ppermute(bwd, "crop", bwd_perm)
            got.append((fwd, ring_arr[(pos - k) % ncrop], 0, wrows))
            got.append((bwd, ring_arr[(pos + k) % ncrop], 0, wrows))
        if steps_fwd > steps_bwd:
            src = ring_arr[(pos - steps_fwd) % ncrop]
            got.append((lax.ppermute(fwd[:split], "crop", fwd_perm), src, 0, split))
            got.append((lax.ppermute(bwd[split:], "crop", bwd_perm), src, split, wrows - split))
        return got

    kv_got = ring_pieces(lax.optimization_barrier(jnp.concatenate([key_weight, value_weight], axis=1)))
    q_piece, last_a, last_b = lax.optimization_barrier(
        (query_weight, kv_got[-1][0], kv_got[-2][0])
    )
    kv_got[-1] = (last_a,) + kv_got[-1][1:]
    kv_got[-2] = (last_b,) + kv_got[-2][1:]
    tokens_in = head_gather(delivered)
    kv_weight = jnp.concatenate([p for p, _, _, _ in kv_got], axis=0)
    tokens_perm = jnp.concatenate(
        [lax.dynamic_slice_in_dim(tokens_in, src * wrows + lo, n, 1) for _, src, lo, n in kv_got],
        axis=1,
    )
    kv = jnp.dot(tokens_perm, kv_weight, preferred_element_type=jnp.float32).astype(jnp.bfloat16)
    incoming = kv.reshape(ncrop, CAP, CT, 2 * width)

    def q_part(acc, piece, src, lo, n):
        cols = lax.dynamic_slice_in_dim(queries_in, src * wrows + lo, n, 1)
        return lax.optimization_barrier(acc + jnp.dot(cols, piece, preferred_element_type=jnp.float32))

    acc = q_part(jnp.zeros((queries_in.shape[0], width), jnp.float32), q_piece, me, 0, wrows)
    fwd = q_piece
    bwd = q_piece
    for k in range(1, steps_bwd + 1):
        fwd = lax.ppermute(fwd, "crop", fwd_perm)
        bwd = lax.ppermute(bwd, "crop", bwd_perm)
        acc = q_part(acc, fwd, ring_arr[(pos - k) % ncrop], 0, wrows)
        acc = q_part(acc, bwd, ring_arr[(pos + k) % ncrop], 0, wrows)
    if steps_fwd > steps_bwd:
        src = ring_arr[(pos - steps_fwd) % ncrop]
        acc = q_part(acc, lax.ppermute(fwd[:split], "crop", fwd_perm), src, 0, split)
        acc = q_part(acc, lax.ppermute(bwd[split:], "crop", bwd_perm), src, split, wrows - split)
    query = acc.astype(jnp.bfloat16)
    nslots = ncrop * CAP
    keys_all = incoming[..., :width].reshape(nslots * CT, heads_here, HD)
    vals_all = incoming[..., width:].reshape(nslots * CT, heads_here, HD)
    query_row = query.reshape(rows_here, GR, heads_here, HD)
    in_use = (jnp.arange(NB, dtype=jnp.int32)[None, :] < region_len[:, None])[:, :, None]
    hits = region_slots[:, :, None] == jnp.arange(nslots, dtype=jnp.int32)[None, None, :]
    member = jnp.any(hits & in_use, axis=1)
    member = jnp.repeat(member, CT, axis=1)
    scale = 1.0 / HD**0.5
    scores = (
        jnp.einsum("rghe,khe->rghk", query_row, keys_all, preferred_element_type=jnp.float32)
        * scale
    )
    scores = jnp.where(member[:, None, None, :], scores, jnp.float32(-1e30))
    top = jnp.max(scores, axis=-1, keepdims=True)
    expo = jnp.exp(scores - top)
    weights = (expo / jnp.sum(expo, axis=-1, keepdims=True)).astype(jnp.bfloat16)
    result = jnp.einsum("rghk,khe->rghe", weights, vals_all, preferred_element_type=jnp.float32)
    return result.astype(jnp.bfloat16).reshape(rows_here * GR, width)


def solution(mesh):
    placed = (
        P("crop", "head"),
        P("crop", "head"),
        P("crop", "head"),
        P("crop", "head"),
        P("crop", "head"),
        P("crop", None, None),
        P("crop", None),
        P("crop"),
    )
    return jax.shard_map(
        body, mesh=mesh, in_specs=placed, out_specs=P("crop", "head"), check_vma=False
    )
```
